256 devices in a mesh: lon: 64 (over x_hi, z, y), lat: 4 (over x_lo, core).
Axes of the slice: x: 4 (x_hi: 2, x_lo: 2; x = x_hi * 2 + x_lo), y: 4, z: 8, core: 2. Of those that a mesh axis runs over, the one named last changes fastest.
Arguments:
- adjoint_final: float32 [10, 256, 16384], P(None, 'lat', 'lon'), may hold values from -6 to 6
- stored_tracer: float32 [4, 10, 256, 16384], P(None, None, 'lat', 'lon'), may hold values from -4 to 4
- stored_zonal: float32 [4, 10, 256, 16384], P(None, None, 'lat', 'lon'), may hold values from -4 to 4
- stored_meridional: float32 [4, 10, 256, 16384], P(None, None, 'lat', 'lon'), may hold values from -4 to 4
- diffusivity: float32 [256, 16384], P('lat', 'lon'), may hold values from 0.02 to 0.2
- level_mixing: float32 [10, 10], replicated, may hold values from -2 to 2
- wet_tiles: int32 [4, 128], P('lat', 'lon'), may hold values 0 or 1
- state_index: int32 [2], replicated, may hold values from 0 to 3, as said below
Outputs:
- adjoint_start: float32 [10, 256, 16384], P(None, 'lat', 'lon')
The draws below stay inside these ranges and needn't reach their ends.
Inputs may be any that keep to these rules, and one draw needn't show every extreme that they name: The entries of state_index are distinct stored states, and one of them is the last stored state.
All inputs are finite; a program needn't handle non-finite values. No bound on the sum of `wet_tiles` on one device may be relied on, other than what follows from the above.
Results may differ from the reference program's by a relative error of at most 0.0001.
Values sent between devices are 32-bit elements; how exact they have to be, the bound alone decides.
No kernel may reach another device: no remote copies, remote signals or barrier semaphores. Data moves between devices by JAX's collectives and lax.ppermute only.
A program may use at most 64 MiB of HBM per device.

```python
import math
import jax
import jax.numpy as jnp
from jax import lax

LEV = 10
TLAT = 64
TLON = 128
STEPS = 2
STORE = 4
NLON = 16384
NLAT = 256
NTLON = 128
N_LAT = 4


def draw_state_index(key, part):
    others = jax.random.permutation(jax.random.fold_in(key, 11), STORE - 1)[:STEPS - 1].astype(jnp.int32)
    values = jnp.concatenate([others, jnp.full((1,), STORE - 1, jnp.int32)])
    order = jax.random.permutation(jax.random.fold_in(key, 13), STEPS)
    return values[order].astype(jnp.int32)


def with_ends(array, own_key, least, high):
    place = [jax.random.randint(jax.random.fold_in(own_key, axis), (), 0, length) for axis, length in enumerate(array.shape)]
    widest = array.shape.index(max(array.shape))
    next_to = place[:widest] + [(place[widest] + 1) % array.shape[widest]] + place[widest + 1:]
    return array.at[tuple(place)].set(least).at[tuple(next_to)].set(high)


def shard_levels(stream_key, shape, pieces, low, top_value):
    def one(dim, shards_of):
        steps = jax.random.uniform(jax.random.fold_in(jax.random.fold_in(stream_key, 6), dim), (shards_of,), jnp.float32, low / len(pieces), top_value / len(pieces))
        return jnp.repeat(jnp.exp(steps), shape[dim] // shards_of).reshape((-1,) + (1,) * (len(shape) - dim - 1))

    factor_of = one(*pieces[0])
    for cut in pieces[1:]:
        factor_of = factor_of * one(*cut)
    return factor_of


def scatter_about(key, extent, scale, limit, shards=(), kind=jnp.bfloat16):
    factor_of = shard_levels(key, extent, shards, -0.22, 0.18) if shards else 1.0
    array = jax.random.normal(key, extent, jnp.float32) * scale * factor_of
    return jnp.minimum(jnp.maximum(array, -limit), limit).astype(kind)


def setup_inputs(seed: int = 0) -> dict:
    seeds = jax.random.split(jax.random.key(seed), 9)
    return {
        "adjoint_final": scatter_about(seeds[0], (LEV, NLAT, NLON), 1.0, 6.0, ((1, 4), (2, 64)), jnp.float32),
        "stored_tracer": scatter_about(seeds[1], (STORE, LEV, NLAT, NLON), 1.0, 4.0, ((2, 4), (3, 64)), jnp.float32),
        "stored_zonal": scatter_about(seeds[2], (STORE, LEV, NLAT, NLON), 1.0, 4.0, ((2, 4), (3, 64)), jnp.float32),
        "stored_meridional": scatter_about(seeds[3], (STORE, LEV, NLAT, NLON), 1.0, 4.0, ((2, 4), (3, 64)), jnp.float32),
        "diffusivity": jnp.clip(jnp.exp(math.log(0.2) - 2.3025851 * jax.random.uniform(seeds[4], (NLAT, NLON), jnp.float32) ** shard_levels(seeds[4], (NLAT, NLON), ((0, 4), (1, 64)), -0.2, 0.2)), 0.02, 0.2),
        "level_mixing": scatter_about(seeds[5], (LEV, LEV), LEV ** -0.5, 2.0, (), jnp.float32),
        "wet_tiles": with_ends((jax.random.randint(seeds[6], (N_LAT, NTLON), 0, 4) < 3).astype(jnp.int32), jax.random.fold_in(seeds[6], 1), 0, 1),
        "state_index": draw_state_index(jax.random.fold_in(seeds[8], 71), 0),
    }


advect_scale = 0.25
damping = 0.3


def east_of(field):
    return jnp.roll(field, -1, 2)


def west_of(field):
    return jnp.roll(field, 1, 2)


def north_of(field):
    return jnp.concatenate([field[:, 1:, :], field[:, -1:, ::-1]], axis=1)


def south_of(field):
    return jnp.concatenate([jnp.zeros_like(field[:, :1, :]), field[:, :-1, :]], axis=1)


def reference(adjoint_final, stored_tracer, stored_zonal, stored_meridional, diffusivity, level_mixing, wet_tiles, state_index):
    wet = jnp.repeat(jnp.repeat(wet_tiles, TLAT, 0), TLON, 1).astype(jnp.float32)[None]
    adjoint = adjoint_final * wet
    for back in range(STEPS):
        chosen = state_index[STEPS - 1 - back]
        tracer = stored_tracer[chosen]
        zonal = stored_zonal[chosen]
        merid = stored_meridional[chosen]
        spread = diffusivity[None] * adjoint
        zonal_flux = zonal * adjoint
        merid_flux = merid * adjoint
        nearby = east_of(spread) + west_of(spread) + north_of(spread) + south_of(spread)
        advect = east_of(zonal_flux) - west_of(zonal_flux) + north_of(merid_flux) - south_of(merid_flux)
        vertical = jnp.einsum("ml,mab->lab", level_mixing, adjoint, precision=lax.Precision.HIGHEST)
        adjoint = wet * (adjoint - 4.0 * spread + nearby + advect_scale * advect + vertical - damping * tracer * tracer * adjoint)
    return adjoint
```

```python
import functools

import jax
import jax.numpy as jnp
from jax import lax
from jax.experimental import pallas as pl
from jax.experimental.pallas import tpu as pltpu
from jax.sharding import PartitionSpec as P

TLON = 128
STEPS = 2


advect_scale = 0.25
damping = 0.3


def shift_pairs(count, delta, periodic):
    pairs = []
    for i in range(count):
        j = i + delta
        if periodic:
            pairs.append((i, j % count))
        elif 0 <= j < count:
            pairs.append((i, j))
    return pairs


def as_column(row, size):
    spread_rows = jnp.broadcast_to(row, (size, size))
    r = lax.broadcasted_iota(jnp.int32, (size, size), 0)
    c = lax.broadcasted_iota(jnp.int32, (size, size), 1)
    return jnp.sum(jnp.where(r == c, spread_rows, 0.0), axis=1, keepdims=True)


def step_kernel(
    first,
    si_ref,
    wt_ref,
    flag_ref,
    lm_ref,
    adj_ref,
    d_ref,
    t_ref,
    u_ref,
    v_ref,
    he_ref,
    hw_ref,
    hn_ref,
    hf_ref,
    hs_ref,
    out_ref,
):
    del si_ref
    l = pl.program_id(0)
    levels, rows, width = adj_ref.shape
    lane = lax.broadcasted_iota(jnp.int32, (rows, width), 1)
    row = lax.broadcasted_iota(jnp.int32, (rows, width), 0)

    wet_i = jnp.zeros((rows, width), jnp.int32)
    for t in range(width // TLON):
        inside = (lane >= t * TLON) & (lane < (t + 1) * TLON)
        wet_i = jnp.where(inside, wt_ref[t], wet_i)
    wet = wet_i.astype(jnp.float32)

    def level(m):
        a_m = adj_ref[m]
        return a_m * wet if first else a_m

    a = level(l)
    vertical = lm_ref[0, l] * level(0)
    for m in range(1, levels):
        vertical = vertical + lm_ref[m, l] * level(m)

    s = d_ref[...] * a
    zf = u_ref[...] * a
    mf = v_ref[...] * a
    east_src = s + advect_scale * zf
    west_src = s - advect_scale * zf
    north_src = s + advect_scale * mf
    south_src = s - advect_scale * mf

    east_col = as_column(he_ref[pl.ds(l, 1), :], rows)
    west_col = as_column(hw_ref[pl.ds(l, 1), :], rows)
    top = flag_ref[0] == 1
    north_row = jnp.where(top, hf_ref[pl.ds(l, 1), :], hn_ref[pl.ds(l, 1), :])
    south_row = hs_ref[pl.ds(l, 1), :]

    east = jnp.where(lane == width - 1, east_col, pltpu.roll(east_src, width - 1, 1))
    west = jnp.where(lane == 0, west_col, pltpu.roll(west_src, 1, 1))
    north = jnp.where(row == rows - 1, north_row, pltpu.roll(north_src, rows - 1, 0))
    south = jnp.where(row == 0, south_row, pltpu.roll(south_src, 1, 0))

    t = t_ref[...]
    out_ref[...] = wet * (
        a - 4.0 * s + east + west + north + south + vertical - damping * t * t * a
    )


def run_step(k, first, si, wt, flags, lm, adj, d, tracer, zonal, merid, he, hw, hn, hf, hs):
    levels, rows, width = adj.shape
    full3 = pl.BlockSpec((levels, rows, width), lambda l, *_: (0, 0, 0))
    full2 = pl.BlockSpec((rows, width), lambda l, *_: (0, 0))
    state = pl.BlockSpec((None, None, rows, width), lambda l, si, *_: (si[k], l, 0, 0))
    lon_halo = pl.BlockSpec((levels, rows), lambda l, *_: (0, 0))
    lat_halo = pl.BlockSpec((levels, width), lambda l, *_: (0, 0))
    n = levels * rows * width
    return pl.pallas_call(
        functools.partial(step_kernel, first),
        out_shape=jax.ShapeDtypeStruct(adj.shape, jnp.float32),
        grid_spec=pltpu.PrefetchScalarGridSpec(
            num_scalar_prefetch=3,
            grid=(levels,),
            in_specs=[
                pl.BlockSpec(memory_space=pltpu.SMEM),
                full3,
                full2,
                state,
                state,
                state,
                lon_halo,
                lon_halo,
                lat_halo,
                lat_halo,
                lat_halo,
            ],
            out_specs=pl.BlockSpec((None, rows, width), lambda l, *_: (l, 0, 0)),
        ),
        cost_estimate=pl.CostEstimate(flops=60 * n, bytes_accessed=24 * n, transcendentals=0),
    )(si, wt, flags, lm, adj, d, tracer, zonal, merid, he, hw, hn, hf, hs)


def shards(
    adjoint_final,
    stored_tracer,
    stored_zonal,
    stored_meridional,
    diffusivity,
    level_mixing,
    wet_tiles,
    state_index,
):
    n_lat = lax.axis_size("lat")
    n_lon = lax.axis_size("lon")
    levels, rows, width = adjoint_final.shape
    wt = wet_tiles.reshape(-1)
    wet_row = jnp.repeat(wt, TLON).astype(jnp.float32)
    is_top = lax.axis_index("lat") == n_lat - 1
    flags = is_top.astype(jnp.int32).reshape(1)

    to_west = shift_pairs(n_lon, -1, True)
    to_east = shift_pairs(n_lon, 1, True)
    to_south = shift_pairs(n_lat, -1, False)
    to_north = shift_pairs(n_lat, 1, False)
    top = n_lat - 1
    fold = [(j * n_lat + top, (n_lon - 1 - j) * n_lat + top) for j in range(n_lon)]

    adj = adjoint_final
    for back in range(STEPS):
        k = STEPS - 1 - back
        first = back == 0
        chosen = state_index[k]
        a = adj * wet_row if first else adj
        zonal = lax.dynamic_index_in_dim(stored_zonal, chosen, 0, keepdims=False)
        merid = lax.dynamic_index_in_dim(stored_meridional, chosen, 0, keepdims=False)
        a_w, a_e = a[:, :, 0], a[:, :, width - 1]
        a_s, a_n = a[:, 0, :], a[:, rows - 1, :]
        east_payload = diffusivity[:, 0] * a_w + advect_scale * (zonal[:, :, 0] * a_w)
        west_payload = diffusivity[:, width - 1] * a_e - advect_scale * (zonal[:, :, width - 1] * a_e)
        north_payload = diffusivity[0] * a_s + advect_scale * (merid[:, 0, :] * a_s)
        south_payload = diffusivity[rows - 1] * a_n - advect_scale * (merid[:, rows - 1, :] * a_n)
        fold_payload = (diffusivity[rows - 1] * a_n + advect_scale * (merid[:, rows - 1, :] * a_n))[:, ::-1]

        he = lax.ppermute(east_payload, "lon", to_west)
        hw = lax.ppermute(west_payload, "lon", to_east)
        hn = lax.ppermute(north_payload, "lat", to_south)
        hs = lax.ppermute(south_payload, "lat", to_north)
        hf = lax.ppermute(fold_payload, ("lon", "lat"), fold)
        adj = run_step(
            k, first, state_index, wt, flags, level_mixing, adj, diffusivity,
            stored_tracer, stored_zonal, stored_meridional, he, hw, hn, hf, hs,
        )
    return adj


def solution(mesh):
    return jax.shard_map(
        shards,
        mesh=mesh,
        in_specs=(
            P(None, "lat", "lon"),
            P(None, None, "lat", "lon"),
            P(None, None, "lat", "lon"),
            P(None, None, "lat", "lon"),
            P("lat", "lon"),
            P(),
            P("lat", "lon"),
            P(),
        ),
        out_specs=P(None, "lat", "lon"),
        check_vma=False,
    )
```

```python
import functools

import jax
import jax.numpy as jnp
from jax import lax
from jax.experimental import pallas as pl
from jax.experimental.pallas import tpu as pltpu
from jax.sharding import PartitionSpec as P

TLON = 128
STEPS = 2


advect_scale = 0.25
damping = 0.3


def shift_pairs(count, delta, periodic):
    pairs = []
    for i in range(count):
        j = i + delta
        if periodic:
            pairs.append((i, j % count))
        elif 0 <= j < count:
            pairs.append((i, j))
    return pairs


def wet_field(wt_ref, rows, width):
    lane = lax.broadcasted_iota(jnp.int32, (rows, width), 1)
    wet_i = jnp.zeros((rows, width), jnp.int32)
    for t in range(width // TLON):
        inside = (lane >= t * TLON) & (lane < (t + 1) * TLON)
        wet_i = jnp.where(inside, wt_ref[t], wet_i)
    return wet_i.astype(jnp.float32)


class Payload:
    def __init__(self, levels, rows, width):
        self.levels = levels
        self.rows = rows
        self.width = width
        self.lane = lax.broadcasted_iota(jnp.int32, (rows, TLON), 1)
        self.east = jnp.zeros((rows, TLON), jnp.float32)
        self.west = jnp.zeros((rows, TLON), jnp.float32)

    def add(self, l, a, d, u, v, pn_ref, ps_ref, pf_ref):
        rows, width = self.rows, self.width
        a_w, a_e = a[:, 0:1], a[:, width - 1:width]
        east = d[:, 0:1] * a_w + advect_scale * (u[:, 0:1] * a_w)
        west = d[:, width - 1:width] * a_e - advect_scale * (u[:, width - 1:width] * a_e)
        self.east = jnp.where(self.lane == l, jnp.broadcast_to(east, (rows, TLON)), self.east)
        self.west = jnp.where(self.lane == l, jnp.broadcast_to(west, (rows, TLON)), self.west)
        a_s, a_n = a[0:1, :], a[rows - 1:rows, :]
        pn_ref[l:l + 1, :] = d[0:1, :] * a_s + advect_scale * (v[0:1, :] * a_s)
        s_n = d[rows - 1:rows, :] * a_n
        m_n = v[rows - 1:rows, :] * a_n
        ps_ref[l:l + 1, :] = s_n - advect_scale * m_n
        pf_ref[l:l + 1, :] = s_n + advect_scale * m_n

    def finish(self, pe_ref, pw_ref):
        pe_ref[...] = self.east[:, : self.levels]
        pw_ref[...] = self.west[:, : self.levels]


def prologue_kernel(si_ref, wt_ref, af_ref, d_ref, u_ref, v_ref, pe_ref, pw_ref, pn_ref, ps_ref, pf_ref):
    del si_ref
    levels, rows, width = af_ref.shape
    wet = wet_field(wt_ref, rows, width)
    d = d_ref[...]
    out = Payload(levels, rows, width)
    for l in range(levels):
        out.add(l, af_ref[l] * wet, d, u_ref[l], v_ref[l], pn_ref, ps_ref, pf_ref)
    out.finish(pe_ref, pw_ref)


def step_kernel(first, emit, si_ref, wt_ref, flag_ref, lm_ref, adj_ref, d_ref, t_ref, u_ref, v_ref,
                he_ref, hw_ref, hn_ref, hf_ref, hs_ref, *rest):
    del si_ref
    if emit:
        u2_ref, v2_ref, out_ref, pe_ref, pw_ref, pn_ref, ps_ref, pf_ref, a_ref = rest
    else:
        out_ref, a_ref = rest
    levels, rows, width = adj_ref.shape
    lane = lax.broadcasted_iota(jnp.int32, (rows, width), 1)
    row = lax.broadcasted_iota(jnp.int32, (rows, width), 0)
    wet = wet_field(wt_ref, rows, width)
    if first:
        for m in range(levels):
            a_ref[m] = adj_ref[m] * wet
        src = a_ref
    else:
        src = adj_ref
    d = d_ref[...]
    he = he_ref[...]
    hw = hw_ref[...]
    top = flag_ref[0] == 1
    payload = Payload(levels, rows, width) if emit else None

    for l in range(levels):
        a = src[l]
        vertical = lm_ref[0, l] * src[0]
        for m in range(1, levels):
            vertical = vertical + lm_ref[m, l] * src[m]
        s = d * a
        zf = u_ref[l] * a
        mf = v_ref[l] * a
        east_src = s + advect_scale * zf
        west_src = s - advect_scale * zf
        north_src = s + advect_scale * mf
        south_src = s - advect_scale * mf

        east_col = jnp.broadcast_to(he[:, l:l + 1], (rows, width))
        west_col = jnp.broadcast_to(hw[:, l:l + 1], (rows, width))
        north_row = jnp.where(top, hf_ref[l:l + 1, :], hn_ref[l:l + 1, :])
        south_row = hs_ref[l:l + 1, :]

        east = jnp.where(lane == width - 1, east_col, pltpu.roll(east_src, width - 1, 1))
        west = jnp.where(lane == 0, west_col, pltpu.roll(west_src, 1, 1))
        north = jnp.where(row == rows - 1, north_row, pltpu.roll(north_src, rows - 1, 0))
        south = jnp.where(row == 0, south_row, pltpu.roll(south_src, 1, 0))

        t = t_ref[l]
        new = wet * (a - 4.0 * s + east + west + north + south + vertical - damping * t * t * a)
        out_ref[l] = new
        if emit:
            payload.add(l, new, d, u2_ref[l], v2_ref[l], pn_ref, ps_ref, pf_ref)
    if emit:
        payload.finish(pe_ref, pw_ref)


def payload_shapes(levels, rows, width):
    lon = jax.ShapeDtypeStruct((rows, levels), jnp.float32)
    lat = jax.ShapeDtypeStruct((levels, width), jnp.float32)
    return [lon, lon, lat, lat, lat]


def whole(shape):
    return pl.BlockSpec(shape, lambda i, *_: (0,) * len(shape))


def state_spec(k, levels, rows, width):
    return pl.BlockSpec((None, levels, rows, width), lambda i, si, *_: (si[k], 0, 0, 0))


def run_prologue(k, si, wt, af, d, zonal, merid):
    levels, rows, width = af.shape
    shapes = payload_shapes(levels, rows, width)
    n = levels * rows * width
    return pl.pallas_call(
        prologue_kernel,
        out_shape=shapes,
        grid_spec=pltpu.PrefetchScalarGridSpec(
            num_scalar_prefetch=2,
            grid=(1,),
            in_specs=[whole(af.shape), whole(d.shape), state_spec(k, levels, rows, width),
                      state_spec(k, levels, rows, width)],
            out_specs=[whole(s.shape) for s in shapes],
        ),
        cost_estimate=pl.CostEstimate(flops=2 * n, bytes_accessed=12 * n, transcendentals=0),
    )(si, wt, af, d, zonal, merid)


def run_step(k, k_next, si, wt, flags, lm, adj, d, tracer, zonal, merid, he, hw, hn, hf, hs):
    levels, rows, width = adj.shape
    first = k_next is not None
    emit = k_next is not None
    state = state_spec(k, levels, rows, width)
    in_specs = [
        pl.BlockSpec(memory_space=pltpu.SMEM),
        whole(adj.shape), whole(d.shape), state, state, state,
        whole(he.shape), whole(hw.shape), whole(hn.shape), whole(hf.shape), whole(hs.shape),
    ]
    args = [si, wt, flags, lm, adj, d, tracer, zonal, merid, he, hw, hn, hf, hs]
    out_shape = [jax.ShapeDtypeStruct(adj.shape, jnp.float32)]
    if emit:
        nxt = state_spec(k_next, levels, rows, width)
        in_specs += [nxt, nxt]
        args += [zonal, merid]
        out_shape += payload_shapes(levels, rows, width)
    n = levels * rows * width
    outs = pl.pallas_call(
        functools.partial(step_kernel, first, emit),
        out_shape=out_shape,
        grid_spec=pltpu.PrefetchScalarGridSpec(
            num_scalar_prefetch=3,
            grid=(1,),
            in_specs=in_specs,
            out_specs=[whole(s.shape) for s in out_shape],
            scratch_shapes=[pltpu.VMEM((levels, rows, width), jnp.float32)],
        ),
        cost_estimate=pl.CostEstimate(flops=60 * n, bytes_accessed=32 * n, transcendentals=0),
    )(*args)
    return outs[0], outs[1:]


def shards(
    adjoint_final,
    stored_tracer,
    stored_zonal,
    stored_meridional,
    diffusivity,
    level_mixing,
    wet_tiles,
    state_index,
):
    n_lat = lax.axis_size("lat")
    n_lon = lax.axis_size("lon")
    wt = wet_tiles.reshape(-1)
    is_top = lax.axis_index("lat") == n_lat - 1
    flags = is_top.astype(jnp.int32).reshape(1)

    to_west = shift_pairs(n_lon, -1, True)
    to_east = shift_pairs(n_lon, 1, True)
    to_south = shift_pairs(n_lat, -1, False)
    to_north = shift_pairs(n_lat, 1, False)
    top = n_lat - 1
    fold = [(j * n_lat + top, (n_lon - 1 - j) * n_lat + top) for j in range(n_lon)]

    def exchange(payloads):
        pe, pw, pn, ps, pf = payloads
        he = lax.ppermute(pe, "lon", to_west)
        hw = lax.ppermute(pw, "lon", to_east)
        hn = lax.ppermute(pn, "lat", to_south)
        hs = lax.ppermute(ps, "lat", to_north)
        hf = lax.ppermute(pf[:, ::-1], ("lon", "lat"), fold)
        return he, hw, hn, hf, hs

    payloads = run_prologue(STEPS - 1, state_index, wt, adjoint_final, diffusivity,
                            stored_zonal, stored_meridional)
    adj = adjoint_final
    for back in range(STEPS):
        k = STEPS - 1 - back
        k_next = k - 1 if k > 0 else None
        halos = exchange(payloads)
        adj, payloads = run_step(
            k, k_next, state_index, wt, flags, level_mixing, adj, diffusivity,
            stored_tracer, stored_zonal, stored_meridional, *halos,
        )
    return adj


def solution(mesh):
    return jax.shard_map(
        shards,
        mesh=mesh,
        in_specs=(
            P(None, "lat", "lon"),
            P(None, None, "lat", "lon"),
            P(None, None, "lat", "lon"),
            P(None, None, "lat", "lon"),
            P("lat", "lon"),
            P(),
            P("lat", "lon"),
            P(),
        ),
        out_specs=P(None, "lat", "lon"),
        check_vma=False,
    )
```

```python
import functools

import jax
import jax.numpy as jnp
from jax import lax
from jax.experimental import pallas as pl
from jax.experimental.pallas import tpu as pltpu
from jax.sharding import PartitionSpec as P

TLON = 128
STEPS = 2


advect_scale = 0.25
damping = 0.3


def shift_pairs(count, delta, periodic):
    pairs = []
    for i in range(count):
        j = i + delta
        if periodic:
            pairs.append((i, j % count))
        elif 0 <= j < count:
            pairs.append((i, j))
    return pairs


def wet_field(wt_ref, rows, width):
    lane = lax.broadcasted_iota(jnp.int32, (rows, width), 1)
    wet_i = jnp.zeros((rows, width), jnp.int32)
    for t in range(width // TLON):
        inside = (lane >= t * TLON) & (lane < (t + 1) * TLON)
        wet_i = jnp.where(inside, wt_ref[t], wet_i)
    return wet_i.astype(jnp.float32)


def reverse_lanes(x):
    width = x.shape[-1]
    i = lax.broadcasted_iota(jnp.int32, (width, width), 0)
    j = lax.broadcasted_iota(jnp.int32, (width, width), 1)
    flip = jnp.where(i + j == width - 1, 1.0, 0.0).astype(jnp.bfloat16)
    x1 = x.astype(jnp.bfloat16)
    r1 = x - x1.astype(jnp.float32)
    x2 = r1.astype(jnp.bfloat16)
    x3 = (r1 - x2.astype(jnp.float32)).astype(jnp.bfloat16)

    def perm(part):
        return jnp.dot(part, flip, preferred_element_type=jnp.float32)

    return (perm(x1) + perm(x2)) + perm(x3)


class Collector:
    def __init__(self, levels, rows, width, reverse_fold):
        self.levels = levels
        self.rows = rows
        self.width = width
        self.reverse_fold = reverse_fold
        self.lane = lax.broadcasted_iota(jnp.int32, (rows, TLON), 1)
        self.row = lax.broadcasted_iota(jnp.int32, (16, width), 0)
        self.cols = [jnp.zeros((rows, TLON), jnp.float32) for _ in range(2)]
        self.rows_acc = [jnp.zeros((16, width), jnp.float32) for _ in range(3)]

    def add(self, l, east, west, north, south, fold):
        for i, col in enumerate((east, west)):
            wide = jnp.broadcast_to(col, (self.rows, TLON))
            self.cols[i] = jnp.where(self.lane == l, wide, self.cols[i])
        for i, line in enumerate((north, south, fold)):
            tall = jnp.broadcast_to(line, (16, self.width))
            self.rows_acc[i] = jnp.where(self.row == l, tall, self.rows_acc[i])

    def finish(self, pe_ref, pw_ref, pn_ref, ps_ref, pf_ref):
        levels = self.levels
        pe_ref[...] = self.cols[0][:, :levels]
        pw_ref[...] = self.cols[1][:, :levels]
        pn_ref[...] = self.rows_acc[0][:levels]
        ps_ref[...] = self.rows_acc[1][:levels]
        fold = self.rows_acc[2]
        if self.reverse_fold:
            fold = reverse_lanes(fold)
        pf_ref[...] = fold[:levels]


def coefficients(l, d, u, v, rows, width):
    return (
        d[:, 0:1] + advect_scale * u[:, 0:1],
        d[:, width - 1:width] - advect_scale * u[:, width - 1:width],
        d[0:1, :] + advect_scale * v[0:1, :],
        d[rows - 1:rows, :] - advect_scale * v[rows - 1:rows, :],
        d[rows - 1:rows, :] + advect_scale * v[rows - 1:rows, :],
    )


def edge_values(ce, cw, cn, cs, cf, a, rows, width):
    return (
        ce * a[:, 0:1],
        cw * a[:, width - 1:width],
        cn * a[0:1, :],
        cs * a[rows - 1:rows, :],
        cf * a[rows - 1:rows, :],
    )


def prologue_kernel(si_ref, wt_ref, af_ref, d_ref, u_ref, v_ref, pe_ref, pw_ref, pn_ref, ps_ref, pf_ref):
    del si_ref
    levels, rows, width = af_ref.shape
    wet = wet_field(wt_ref, rows, width)
    d = d_ref[...]
    out = Collector(levels, rows, width, True)
    for l in range(levels):
        coef = coefficients(l, d, u_ref[l], v_ref[l], rows, width)
        out.add(l, *edge_values(*coef, af_ref[l] * wet, rows, width))
    out.finish(pe_ref, pw_ref, pn_ref, ps_ref, pf_ref)


def core_kernel(first, emit, si_ref, wt_ref, lm_ref, adj_ref, d_ref, t_ref, u_ref, v_ref, *rest):
    del si_ref
    if emit:
        u2_ref, v2_ref, out_ref, ce_ref, cw_ref, cn_ref, cs_ref, cf_ref, a_ref = rest
    else:
        out_ref, a_ref = rest
    levels, rows, width = adj_ref.shape
    lane = lax.broadcasted_iota(jnp.int32, (rows, width), 1)
    row = lax.broadcasted_iota(jnp.int32, (rows, width), 0)
    wet = wet_field(wt_ref, rows, width)
    if first:
        for m in range(levels):
            a_ref[m] = adj_ref[m] * wet
        src = a_ref
    else:
        src = adj_ref
    d = d_ref[...]
    coef = Collector(levels, rows, width, False) if emit else None

    for l in range(levels):
        a = src[l]
        vertical = lm_ref[0, l] * src[0]
        for m in range(1, levels):
            vertical = vertical + lm_ref[m, l] * src[m]
        s = d * a
        zf = u_ref[l] * a
        mf = v_ref[l] * a
        east = jnp.where(lane == width - 1, 0.0, pltpu.roll(s + advect_scale * zf, width - 1, 1))
        west = jnp.where(lane == 0, 0.0, pltpu.roll(s - advect_scale * zf, 1, 1))
        north = jnp.where(row == rows - 1, 0.0, pltpu.roll(s + advect_scale * mf, rows - 1, 0))
        south = jnp.where(row == 0, 0.0, pltpu.roll(s - advect_scale * mf, 1, 0))
        t = t_ref[l]
        out_ref[l] = wet * (a - 4.0 * s + east + west + north + south + vertical - damping * t * t * a)
        if emit:
            coef.add(l, *coefficients(l, d, u2_ref[l], v2_ref[l], rows, width))
    if emit:
        coef.finish(ce_ref, cw_ref, cn_ref, cs_ref, cf_ref)


def fix_kernel(emit, wt_ref, flag_ref, part_ref, he_ref, hw_ref, hn_ref, hf_ref, hs_ref, *rest):
    if emit:
        ce_ref, cw_ref, cn_ref, cs_ref, cf_ref, out_ref, pe_ref, pw_ref, pn_ref, ps_ref, pf_ref = rest
    else:
        (out_ref,) = rest
    levels, rows, width = part_ref.shape
    lane = lax.broadcasted_iota(jnp.int32, (rows, width), 1)
    row = lax.broadcasted_iota(jnp.int32, (rows, width), 0)
    wet = wet_field(wt_ref, rows, width)
    he = he_ref[...]
    hw = hw_ref[...]
    top = flag_ref[0] == 1
    if emit:
        ce = ce_ref[...]
        cw = cw_ref[...]
        out = Collector(levels, rows, width, True)
    for l in range(levels):
        north_row = jnp.where(top, hf_ref[l:l + 1, :], hn_ref[l:l + 1, :])
        corr = (
            jnp.where(lane == width - 1, jnp.broadcast_to(he[:, l:l + 1], (rows, width)), 0.0)
            + jnp.where(lane == 0, jnp.broadcast_to(hw[:, l:l + 1], (rows, width)), 0.0)
            + jnp.where(row == rows - 1, north_row, 0.0)
            + jnp.where(row == 0, hs_ref[l:l + 1, :], 0.0)
        )
        new = part_ref[l] + wet * corr
        out_ref[l] = new
        if emit:
            coef = (ce[:, l:l + 1], cw[:, l:l + 1], cn_ref[l:l + 1, :], cs_ref[l:l + 1, :], cf_ref[l:l + 1, :])
            out.add(l, *edge_values(*coef, new, rows, width))
    if emit:
        out.finish(pe_ref, pw_ref, pn_ref, ps_ref, pf_ref)


def payload_shapes(levels, rows, width):
    lon = jax.ShapeDtypeStruct((rows, levels), jnp.float32)
    lat = jax.ShapeDtypeStruct((levels, width), jnp.float32)
    return [lon, lon, lat, lat, lat]


def whole(shape):
    return pl.BlockSpec(shape, lambda i, *_: (0,) * len(shape))


def state_spec(k, levels, rows, width):
    return pl.BlockSpec((None, levels, rows, width), lambda i, si, *_: (si[k], 0, 0, 0))


def run_prologue(k, si, wt, af, d, zonal, merid):
    levels, rows, width = af.shape
    shapes = payload_shapes(levels, rows, width)
    n = levels * rows * width
    return pl.pallas_call(
        prologue_kernel,
        out_shape=shapes,
        grid_spec=pltpu.PrefetchScalarGridSpec(
            num_scalar_prefetch=2,
            grid=(1,),
            in_specs=[whole(af.shape), whole(d.shape), state_spec(k, levels, rows, width),
                      state_spec(k, levels, rows, width)],
            out_specs=[whole(s.shape) for s in shapes],
        ),
        cost_estimate=pl.CostEstimate(flops=2 * n, bytes_accessed=12 * n, transcendentals=0),
    )(si, wt, af, d, zonal, merid)


def run_core(k, k_next, si, wt, lm, adj, d, tracer, zonal, merid):
    levels, rows, width = adj.shape
    first = k_next is not None
    emit = k_next is not None
    state = state_spec(k, levels, rows, width)
    in_specs = [pl.BlockSpec(memory_space=pltpu.SMEM), whole(adj.shape), whole(d.shape), state, state, state]
    args = [si, wt, lm, adj, d, tracer, zonal, merid]
    out_shape = [jax.ShapeDtypeStruct(adj.shape, jnp.float32)]
    if emit:
        nxt = state_spec(k_next, levels, rows, width)
        in_specs += [nxt, nxt]
        args += [zonal, merid]
        out_shape += payload_shapes(levels, rows, width)
    n = levels * rows * width
    outs = pl.pallas_call(
        functools.partial(core_kernel, first, emit),
        out_shape=out_shape,
        grid_spec=pltpu.PrefetchScalarGridSpec(
            num_scalar_prefetch=2,
            grid=(1,),
            in_specs=in_specs,
            out_specs=[whole(s.shape) for s in out_shape],
            scratch_shapes=[pltpu.VMEM((levels, rows, width), jnp.float32)],
        ),
        cost_estimate=pl.CostEstimate(flops=60 * n, bytes_accessed=32 * n, transcendentals=0),
    )(*args)
    return outs[0], outs[1:]


def run_fix(wt, flags, part, halos, coefs):
    levels, rows, width = part.shape
    emit = bool(coefs)
    args = [wt, flags, part, *halos, *coefs]
    in_specs = [whole(x.shape) for x in args[2:]]
    out_shape = [jax.ShapeDtypeStruct(part.shape, jnp.float32)]
    if emit:
        out_shape += payload_shapes(levels, rows, width)
    n = levels * rows * width
    outs = pl.pallas_call(
        functools.partial(fix_kernel, emit),
        out_shape=out_shape,
        grid_spec=pltpu.PrefetchScalarGridSpec(
            num_scalar_prefetch=2,
            grid=(1,),
            in_specs=in_specs,
            out_specs=[whole(s.shape) for s in out_shape],
        ),
        cost_estimate=pl.CostEstimate(flops=10 * n, bytes_accessed=8 * n, transcendentals=0),
    )(*args)
    return outs[0], outs[1:]


def shards(
    adjoint_final,
    stored_tracer,
    stored_zonal,
    stored_meridional,
    diffusivity,
    level_mixing,
    wet_tiles,
    state_index,
):
    n_lat = lax.axis_size("lat")
    n_lon = lax.axis_size("lon")
    wt = wet_tiles.reshape(-1)
    is_top = lax.axis_index("lat") == n_lat - 1
    flags = is_top.astype(jnp.int32).reshape(1)

    to_west = shift_pairs(n_lon, -1, True)
    to_east = shift_pairs(n_lon, 1, True)
    to_south = shift_pairs(n_lat, -1, False)
    to_north = shift_pairs(n_lat, 1, False)
    top = n_lat - 1
    fold = [(j * n_lat + top, (n_lon - 1 - j) * n_lat + top) for j in range(n_lon)]

    def exchange(payloads):
        pe, pw, pn, ps, pf = payloads
        he = lax.ppermute(pe, "lon", to_west)
        hw = lax.ppermute(pw, "lon", to_east)
        hn = lax.ppermute(pn, "lat", to_south)
        hs = lax.ppermute(ps, "lat", to_north)
        hf = lax.ppermute(pf, ("lon", "lat"), fold)
        return he, hw, hn, hf, hs

    payloads = run_prologue(STEPS - 1, state_index, wt, adjoint_final, diffusivity,
                            stored_zonal, stored_meridional)
    adj = adjoint_final
    for back in range(STEPS):
        k = STEPS - 1 - back
        k_next = k - 1 if k > 0 else None
        halos = exchange(payloads)
        part, coefs = run_core(k, k_next, state_index, wt, level_mixing, adj, diffusivity,
                               stored_tracer, stored_zonal, stored_meridional)
        adj, payloads = run_fix(wt, flags, part, halos, coefs)
    return adj


def solution(mesh):
    return jax.shard_map(
        shards,
        mesh=mesh,
        in_specs=(
            P(None, "lat", "lon"),
            P(None, None, "lat", "lon"),
            P(None, None, "lat", "lon"),
            P(None, None, "lat", "lon"),
            P("lat", "lon"),
            P(),
            P("lat", "lon"),
            P(),
        ),
        out_specs=P(None, "lat", "lon"),
        check_vma=False,
    )
```

```python
import functools

import jax
import jax.numpy as jnp
from jax import lax
from jax.experimental import pallas as pl
from jax.experimental.pallas import tpu as pltpu
from jax.sharding import PartitionSpec as P

TLON = 128
STEPS = 2


advect_scale = 0.25
damping = 0.3


def shift_pairs(count, delta, periodic):
    pairs = []
    for i in range(count):
        j = i + delta
        if periodic:
            pairs.append((i, j % count))
        elif 0 <= j < count:
            pairs.append((i, j))
    return pairs


def wet_field(wt_ref, rows, width):
    lane = lax.broadcasted_iota(jnp.int32, (rows, width), 1)
    wet_i = jnp.zeros((rows, width), jnp.int32)
    for t in range(width // TLON):
        inside = (lane >= t * TLON) & (lane < (t + 1) * TLON)
        wet_i = jnp.where(inside, wt_ref[t], wet_i)
    return wet_i.astype(jnp.float32)


def reverse_lanes(x):
    width = x.shape[-1]
    i = lax.broadcasted_iota(jnp.int32, (width, width), 0)
    j = lax.broadcasted_iota(jnp.int32, (width, width), 1)
    flip = jnp.where(i + j == width - 1, 1.0, 0.0).astype(jnp.bfloat16)
    x1 = x.astype(jnp.bfloat16)
    r1 = x - x1.astype(jnp.float32)
    x2 = r1.astype(jnp.bfloat16)
    x3 = (r1 - x2.astype(jnp.float32)).astype(jnp.bfloat16)

    def perm(part):
        return jnp.dot(part, flip, preferred_element_type=jnp.float32)

    return (perm(x1) + perm(x2)) + perm(x3)


class Collector:
    def __init__(self, levels, rows, width, reverse_fold):
        self.levels = levels
        self.rows = rows
        self.width = width
        self.reverse_fold = reverse_fold
        self.lane = lax.broadcasted_iota(jnp.int32, (rows, TLON), 1)
        self.row = lax.broadcasted_iota(jnp.int32, (16, width), 0)
        self.cols = [jnp.zeros((rows, TLON), jnp.float32) for _ in range(2)]
        self.rows_acc = [jnp.zeros((16, width), jnp.float32) for _ in range(3)]

    def add(self, l, east, west, north, south, fold):
        for i, col in enumerate((east, west)):
            wide = jnp.broadcast_to(col, (self.rows, TLON))
            self.cols[i] = jnp.where(self.lane == l, wide, self.cols[i])
        for i, line in enumerate((north, south, fold)):
            tall = jnp.broadcast_to(line, (16, self.width))
            self.rows_acc[i] = jnp.where(self.row == l, tall, self.rows_acc[i])

    def finish(self, pe_ref, pw_ref, pn_ref, ps_ref, pf_ref):
        levels = self.levels
        pe_ref[...] = self.cols[0][:, :levels]
        pw_ref[...] = self.cols[1][:, :levels]
        pn_ref[...] = self.rows_acc[0][:levels]
        ps_ref[...] = self.rows_acc[1][:levels]
        fold = self.rows_acc[2]
        if self.reverse_fold:
            fold = reverse_lanes(fold)
        pf_ref[...] = fold[:levels]

    def finish_pairs(self, flag_ref, pe_ref, pw_ref, pa_ref, pb_ref):
        levels = self.levels
        pe_ref[...] = self.cols[0][:, :levels]
        pw_ref[...] = self.cols[1][:, :levels]
        north_going = self.rows_acc[0][:levels]
        south_going = self.rows_acc[1][:levels]
        fold = reverse_lanes(self.rows_acc[2])[:levels]
        even = flag_ref[0] == 0
        top = flag_ref[1] == 1
        pa_ref[...] = jnp.where(even, south_going, north_going)
        pb_ref[...] = jnp.where(top, fold, jnp.where(even, north_going, south_going))


def coefficients(l, d, u, v, rows, width):
    return (
        d[:, 0:1] + advect_scale * u[:, 0:1],
        d[:, width - 1:width] - advect_scale * u[:, width - 1:width],
        d[0:1, :] + advect_scale * v[0:1, :],
        d[rows - 1:rows, :] - advect_scale * v[rows - 1:rows, :],
        d[rows - 1:rows, :] + advect_scale * v[rows - 1:rows, :],
    )


def edge_values(ce, cw, cn, cs, cf, a, rows, width):
    return (
        ce * a[:, 0:1],
        cw * a[:, width - 1:width],
        cn * a[0:1, :],
        cs * a[rows - 1:rows, :],
        cf * a[rows - 1:rows, :],
    )


def prologue_kernel(si_ref, wt_ref, flag_ref, af_ref, d_ref, u_ref, v_ref, pe_ref, pw_ref, pa_ref, pb_ref):
    del si_ref
    levels, rows, width = af_ref.shape
    wet = wet_field(wt_ref, rows, width)
    d = d_ref[...]
    out = Collector(levels, rows, width, True)
    for l in range(levels):
        coef = coefficients(l, d, u_ref[l], v_ref[l], rows, width)
        out.add(l, *edge_values(*coef, af_ref[l] * wet, rows, width))
    out.finish_pairs(flag_ref, pe_ref, pw_ref, pa_ref, pb_ref)


def core_kernel(first, emit, si_ref, wt_ref, lm_ref, adj_ref, d_ref, t_ref, u_ref, v_ref, *rest):
    del si_ref
    if emit:
        u2_ref, v2_ref, out_ref, ce_ref, cw_ref, cn_ref, cs_ref, cf_ref, a_ref = rest
    else:
        out_ref, a_ref = rest
    levels, rows, width = adj_ref.shape
    lane = lax.broadcasted_iota(jnp.int32, (rows, width), 1)
    row = lax.broadcasted_iota(jnp.int32, (rows, width), 0)
    wet = wet_field(wt_ref, rows, width)
    if first:
        for m in range(levels):
            a_ref[m] = adj_ref[m] * wet
        src = a_ref
    else:
        src = adj_ref
    d = d_ref[...]
    coef = Collector(levels, rows, width, False) if emit else None

    for l in range(levels):
        a = src[l]
        vertical = lm_ref[0, l] * src[0]
        for m in range(1, levels):
            vertical = vertical + lm_ref[m, l] * src[m]
        s = d * a
        zf = u_ref[l] * a
        mf = v_ref[l] * a
        east = jnp.where(lane == width - 1, 0.0, pltpu.roll(s + advect_scale * zf, width - 1, 1))
        west = jnp.where(lane == 0, 0.0, pltpu.roll(s - advect_scale * zf, 1, 1))
        north = jnp.where(row == rows - 1, 0.0, pltpu.roll(s + advect_scale * mf, rows - 1, 0))
        south = jnp.where(row == 0, 0.0, pltpu.roll(s - advect_scale * mf, 1, 0))
        t = t_ref[l]
        out_ref[l] = wet * (a - 4.0 * s + east + west + north + south + vertical - damping * t * t * a)
        if emit:
            coef.add(l, *coefficients(l, d, u2_ref[l], v2_ref[l], rows, width))
    if emit:
        coef.finish(ce_ref, cw_ref, cn_ref, cs_ref, cf_ref)


def fix_kernel(emit, wt_ref, flag_ref, part_ref, he_ref, hw_ref, ha_ref, hb_ref, *rest):
    if emit:
        ce_ref, cw_ref, cn_ref, cs_ref, cf_ref, out_ref, pe_ref, pw_ref, pa_ref, pb_ref = rest
    else:
        (out_ref,) = rest
    levels, rows, width = part_ref.shape
    wet = wet_field(wt_ref, rows, width)
    wet_left, wet_right = wet[:, :TLON], wet[:, width - TLON:]
    wet_bottom, wet_top = wet[0:1, :], wet[rows - 1:rows, :]
    lane = lax.broadcasted_iota(jnp.int32, (rows, TLON), 1)
    he = he_ref[...]
    hw = hw_ref[...]
    even = flag_ref[0] == 0
    if emit:
        ce = ce_ref[...]
        cw = cw_ref[...]
        out = Collector(levels, rows, width, True)
    for l in range(levels):
        x = part_ref[l]
        east = jnp.where(lane == TLON - 1, jnp.broadcast_to(he[:, l:l + 1], (rows, TLON)), 0.0)
        west = jnp.where(lane == 0, jnp.broadcast_to(hw[:, l:l + 1], (rows, TLON)), 0.0)
        out_ref[l] = x
        out_ref[l, :, width - TLON:] = x[:, width - TLON:] + wet_right * east
        out_ref[l, :, :TLON] = out_ref[l, :, :TLON] + wet_left * west
        a_row = ha_ref[l:l + 1, :]
        b_row = hb_ref[l:l + 1, :]
        north_row = jnp.where(even, a_row, b_row)
        south_row = jnp.where(even, b_row, a_row)
        out_ref[l, rows - 1:rows, :] = out_ref[l, rows - 1:rows, :] + wet_top * north_row
        out_ref[l, 0:1, :] = out_ref[l, 0:1, :] + wet_bottom * south_row
        if emit:
            new = out_ref[l]
            coef = (ce[:, l:l + 1], cw[:, l:l + 1], cn_ref[l:l + 1, :], cs_ref[l:l + 1, :], cf_ref[l:l + 1, :])
            out.add(l, *edge_values(*coef, new, rows, width))
    if emit:
        out.finish_pairs(flag_ref, pe_ref, pw_ref, pa_ref, pb_ref)


def payload_shapes(levels, rows, width):
    lon = jax.ShapeDtypeStruct((rows, levels), jnp.float32)
    lat = jax.ShapeDtypeStruct((levels, width), jnp.float32)
    return [lon, lon, lat, lat, lat]


def pair_shapes(levels, rows, width):
    return payload_shapes(levels, rows, width)[:4]


def whole(shape):
    return pl.BlockSpec(shape, lambda i, *_: (0,) * len(shape))


def state_spec(k, levels, rows, width):
    return pl.BlockSpec((None, levels, rows, width), lambda i, si, *_: (si[k], 0, 0, 0))


def run_prologue(k, si, wt, flags, af, d, zonal, merid):
    levels, rows, width = af.shape
    shapes = pair_shapes(levels, rows, width)
    n = levels * rows * width
    return pl.pallas_call(
        prologue_kernel,
        out_shape=shapes,
        grid_spec=pltpu.PrefetchScalarGridSpec(
            num_scalar_prefetch=3,
            grid=(1,),
            in_specs=[whole(af.shape), whole(d.shape), state_spec(k, levels, rows, width),
                      state_spec(k, levels, rows, width)],
            out_specs=[whole(s.shape) for s in shapes],
        ),
        cost_estimate=pl.CostEstimate(flops=2 * n, bytes_accessed=12 * n, transcendentals=0),
    )(si, wt, flags, af, d, zonal, merid)


def run_core(k, k_next, si, wt, lm, adj, d, tracer, zonal, merid):
    levels, rows, width = adj.shape
    first = k_next is not None
    emit = k_next is not None
    state = state_spec(k, levels, rows, width)
    in_specs = [pl.BlockSpec(memory_space=pltpu.SMEM), whole(adj.shape), whole(d.shape), state, state, state]
    args = [si, wt, lm, adj, d, tracer, zonal, merid]
    out_shape = [jax.ShapeDtypeStruct(adj.shape, jnp.float32)]
    if emit:
        nxt = state_spec(k_next, levels, rows, width)
        in_specs += [nxt, nxt]
        args += [zonal, merid]
        out_shape += payload_shapes(levels, rows, width)
    n = levels * rows * width
    outs = pl.pallas_call(
        functools.partial(core_kernel, first, emit),
        out_shape=out_shape,
        grid_spec=pltpu.PrefetchScalarGridSpec(
            num_scalar_prefetch=2,
            grid=(1,),
            in_specs=in_specs,
            out_specs=[whole(s.shape) for s in out_shape],
            scratch_shapes=[pltpu.VMEM((levels, rows, width), jnp.float32)],
        ),
        cost_estimate=pl.CostEstimate(flops=60 * n, bytes_accessed=32 * n, transcendentals=0),
    )(*args)
    return outs[0], outs[1:]


def run_fix(wt, flags, part, halos, coefs):
    levels, rows, width = part.shape
    emit = bool(coefs)
    args = [wt, flags, part, *halos, *coefs]
    in_specs = [whole(x.shape) for x in args[2:]]
    out_shape = [jax.ShapeDtypeStruct(part.shape, jnp.float32)]
    if emit:
        out_shape += pair_shapes(levels, rows, width)
    n = levels * rows * width
    outs = pl.pallas_call(
        functools.partial(fix_kernel, emit),
        out_shape=out_shape,
        grid_spec=pltpu.PrefetchScalarGridSpec(
            num_scalar_prefetch=2,
            grid=(1,),
            in_specs=in_specs,
            out_specs=[whole(s.shape) for s in out_shape],
        ),
        cost_estimate=pl.CostEstimate(flops=10 * n, bytes_accessed=8 * n, transcendentals=0),
    )(*args)
    return outs[0], outs[1:]


def shards(
    adjoint_final,
    stored_tracer,
    stored_zonal,
    stored_meridional,
    diffusivity,
    level_mixing,
    wet_tiles,
    state_index,
):
    n_lat = lax.axis_size("lat")
    n_lon = lax.axis_size("lon")
    wt = wet_tiles.reshape(-1)
    lat_index = lax.axis_index("lat")
    flags = jnp.stack([lat_index % 2, (lat_index == n_lat - 1).astype(jnp.int32)]).astype(jnp.int32)

    to_west = shift_pairs(n_lon, -1, True)
    to_east = shift_pairs(n_lon, 1, True)
    pairs_a = [(i, i ^ 1) for i in range(n_lat)]
    top = n_lat - 1
    pairs_b = []
    for j in range(n_lon):
        for i in range(1, n_lat - 1, 2):
            pairs_b += [(j * n_lat + i, j * n_lat + i + 1), (j * n_lat + i + 1, j * n_lat + i)]
        pairs_b.append((j * n_lat + top, (n_lon - 1 - j) * n_lat + top))

    def exchange(payloads):
        pe, pw, pa, pb = payloads
        he = lax.ppermute(pe, "lon", to_west)
        hw = lax.ppermute(pw, "lon", to_east)
        ha = lax.ppermute(pa, "lat", pairs_a)
        hb = lax.ppermute(pb, ("lon", "lat"), pairs_b)
        return he, hw, ha, hb

    payloads = run_prologue(STEPS - 1, state_index, wt, flags, adjoint_final, diffusivity,
                            stored_zonal, stored_meridional)
    adj = adjoint_final
    for back in range(STEPS):
        k = STEPS - 1 - back
        k_next = k - 1 if k > 0 else None
        halos = exchange(payloads)
        part, coefs = run_core(k, k_next, state_index, wt, level_mixing, adj, diffusivity,
                               stored_tracer, stored_zonal, stored_meridional)
        adj, payloads = run_fix(wt, flags, part, halos, coefs)
    return adj


def solution(mesh):
    return jax.shard_map(
        shards,
        mesh=mesh,
        in_specs=(
            P(None, "lat", "lon"),
            P(None, None, "lat", "lon"),
            P(None, None, "lat", "lon"),
            P(None, None, "lat", "lon"),
            P("lat", "lon"),
            P(),
            P("lat", "lon"),
            P(),
        ),
        out_specs=P(None, "lat", "lon"),
        check_vma=False,
    )
```

```python
import functools

import jax
import jax.numpy as jnp
from jax import lax
from jax.experimental import pallas as pl
from jax.experimental.pallas import tpu as pltpu
from jax.sharding import PartitionSpec as P

TLON = 128
STEPS = 2


advect_scale = 0.25
damping = 0.3


def shift_pairs(count, delta, periodic):
    pairs = []
    for i in range(count):
        j = i + delta
        if periodic:
            pairs.append((i, j % count))
        elif 0 <= j < count:
            pairs.append((i, j))
    return pairs


def wet_field(wt_ref, rows, width):
    lane = lax.broadcasted_iota(jnp.int32, (rows, width), 1)
    wet_i = jnp.zeros((rows, width), jnp.int32)
    for t in range(width // TLON):
        inside = (lane >= t * TLON) & (lane < (t + 1) * TLON)
        wet_i = jnp.where(inside, wt_ref[t], wet_i)
    return wet_i.astype(jnp.float32)


def reverse_lanes(x):
    width = x.shape[-1]
    i = lax.broadcasted_iota(jnp.int32, (width, width), 0)
    j = lax.broadcasted_iota(jnp.int32, (width, width), 1)
    flip = jnp.where(i + j == width - 1, 1.0, 0.0).astype(jnp.bfloat16)
    x1 = x.astype(jnp.bfloat16)
    r1 = x - x1.astype(jnp.float32)
    x2 = r1.astype(jnp.bfloat16)
    x3 = (r1 - x2.astype(jnp.float32)).astype(jnp.bfloat16)

    def perm(part):
        return jnp.dot(part, flip, preferred_element_type=jnp.float32)

    return (perm(x1) + perm(x2)) + perm(x3)


class Collector:
    def __init__(self, levels, rows, width, reverse_fold):
        self.levels = levels
        self.rows = rows
        self.width = width
        self.reverse_fold = reverse_fold
        self.lane = lax.broadcasted_iota(jnp.int32, (rows, TLON), 1)
        self.row = lax.broadcasted_iota(jnp.int32, (16, width), 0)
        self.cols = [jnp.zeros((rows, TLON), jnp.float32) for _ in range(2)]
        self.rows_acc = [jnp.zeros((16, width), jnp.float32) for _ in range(3)]

    def add(self, l, east, west, north, south, fold):
        for i, col in enumerate((east, west)):
            wide = jnp.broadcast_to(col, (self.rows, TLON))
            self.cols[i] = jnp.where(self.lane == l, wide, self.cols[i])
        for i, line in enumerate((north, south, fold)):
            tall = jnp.broadcast_to(line, (16, self.width))
            self.rows_acc[i] = jnp.where(self.row == l, tall, self.rows_acc[i])

    def finish(self, pe_ref, pw_ref, pn_ref, ps_ref, pf_ref):
        levels = self.levels
        pe_ref[...] = self.cols[0][:, :levels]
        pw_ref[...] = self.cols[1][:, :levels]
        pn_ref[...] = self.rows_acc[0][:levels]
        ps_ref[...] = self.rows_acc[1][:levels]
        fold = self.rows_acc[2]
        if self.reverse_fold:
            fold = reverse_lanes(fold)
        pf_ref[...] = fold[:levels]

    def finish_pairs(self, flag_ref, pe_ref, pw_ref, pa_ref, pb_ref):
        levels = self.levels
        pe_ref[...] = self.cols[0][:, :levels]
        pw_ref[...] = self.cols[1][:, :levels]
        north_going = self.rows_acc[0][:levels]
        south_going = self.rows_acc[1][:levels]
        fold = reverse_lanes(self.rows_acc[2])[:levels]
        even = flag_ref[0] == 0
        top = flag_ref[1] == 1
        pa_ref[...] = jnp.where(even, south_going, north_going)
        pb_ref[...] = jnp.where(top, fold, jnp.where(even, north_going, south_going))


def coefficients(l, d, u, v, rows, width):
    return (
        d[:, 0:1] + advect_scale * u[:, 0:1],
        d[:, width - 1:width] - advect_scale * u[:, width - 1:width],
        d[0:1, :] + advect_scale * v[0:1, :],
        d[rows - 1:rows, :] - advect_scale * v[rows - 1:rows, :],
        d[rows - 1:rows, :] + advect_scale * v[rows - 1:rows, :],
    )


def edge_values(ce, cw, cn, cs, cf, a, rows, width):
    return (
        ce * a[:, 0:1],
        cw * a[:, width - 1:width],
        cn * a[0:1, :],
        cs * a[rows - 1:rows, :],
        cf * a[rows - 1:rows, :],
    )


def prologue_kernel(k, si_ref, wt_ref, flag_ref, af_hbm, d_ref, u_hbm, v_hbm, pe_ref, pw_ref, pa_ref, pb_ref,
                    af_buf, u_buf, v_buf, sem):
    levels, rows, width = af_buf.shape
    chosen = si_ref[k]
    copies = []
    for l in range(levels):
        for i, (src, dst) in enumerate(((af_hbm.at[l], af_buf.at[l]), (u_hbm.at[chosen, l], u_buf.at[l]),
                                        (v_hbm.at[chosen, l], v_buf.at[l]))):
            copy = pltpu.make_async_copy(src, dst, sem.at[i, l])
            copy.start()
            copies.append(copy)
    wet = wet_field(wt_ref, rows, width)
    d = d_ref[...]
    out = Collector(levels, rows, width, True)
    for l in range(levels):
        for copy in copies[3 * l:3 * l + 3]:
            copy.wait()
        coef = coefficients(l, d, u_buf[l], v_buf[l], rows, width)
        out.add(l, *edge_values(*coef, af_buf[l] * wet, rows, width))
    out.finish_pairs(flag_ref, pe_ref, pw_ref, pa_ref, pb_ref)


def core_kernel(first, emit, si_ref, wt_ref, lm_ref, adj_ref, d_ref, t_ref, u_ref, v_ref, *rest):
    del si_ref
    if emit:
        u2_ref, v2_ref, out_ref, ce_ref, cw_ref, cn_ref, cs_ref, cf_ref, a_ref = rest
    else:
        out_ref, a_ref = rest
    levels, rows, width = adj_ref.shape
    lane = lax.broadcasted_iota(jnp.int32, (rows, width), 1)
    row = lax.broadcasted_iota(jnp.int32, (rows, width), 0)
    wet = wet_field(wt_ref, rows, width)
    if first:
        for m in range(levels):
            a_ref[m] = adj_ref[m] * wet
        src = a_ref
    else:
        src = adj_ref
    d = d_ref[...]
    coef = Collector(levels, rows, width, False) if emit else None

    for l in range(levels):
        a = src[l]
        vertical = lm_ref[0, l] * src[0]
        for m in range(1, levels):
            vertical = vertical + lm_ref[m, l] * src[m]
        s = d * a
        zf = u_ref[l] * a
        mf = v_ref[l] * a
        east = jnp.where(lane == width - 1, 0.0, pltpu.roll(s + advect_scale * zf, width - 1, 1))
        west = jnp.where(lane == 0, 0.0, pltpu.roll(s - advect_scale * zf, 1, 1))
        north = jnp.where(row == rows - 1, 0.0, pltpu.roll(s + advect_scale * mf, rows - 1, 0))
        south = jnp.where(row == 0, 0.0, pltpu.roll(s - advect_scale * mf, 1, 0))
        t = t_ref[l]
        out_ref[l] = wet * (a - 4.0 * s + east + west + north + south + vertical - damping * t * t * a)
        if emit:
            coef.add(l, *coefficients(l, d, u2_ref[l], v2_ref[l], rows, width))
    if emit:
        coef.finish(ce_ref, cw_ref, cn_ref, cs_ref, cf_ref)


def fix_kernel(emit, n_small, wt_ref, flag_ref, part_hbm, *rest):
    small_hbm = rest[:n_small]
    rest = rest[n_small:]
    if emit:
        out_hbm, pe_ref, pw_ref, pa_ref, pb_ref = rest[:5]
        rest = rest[5:]
    else:
        out_hbm = rest[0]
        rest = rest[1:]
    part_buf, out_buf, in_sem, out_sem = rest
    small = small_hbm
    levels, rows, width = part_buf.shape

    in_copies = [pltpu.make_async_copy(part_hbm.at[l], part_buf.at[l], in_sem.at[l]) for l in range(levels)]
    for c in in_copies:
        c.start()

    wet = wet_field(wt_ref, rows, width)
    wet_left, wet_right = wet[:, :TLON], wet[:, width - TLON:]
    wet_bottom, wet_top = wet[0:1, :], wet[rows - 1:rows, :]
    lane = lax.broadcasted_iota(jnp.int32, (rows, TLON), 1)
    even = flag_ref[0] == 0
    he_ref, hw_ref, ha_ref, hb_ref = small[:4]
    he = he_ref[...]
    hw = hw_ref[...]
    if emit:
        ce_ref, cw_ref, cn_ref, cs_ref, cf_ref = small[4:]
        ce = ce_ref[...]
        cw = cw_ref[...]
        out = Collector(levels, rows, width, True)
    out_copies = []
    for l in range(levels):
        in_copies[l].wait()
        x = part_buf[l]
        east = jnp.where(lane == TLON - 1, jnp.broadcast_to(he[:, l:l + 1], (rows, TLON)), 0.0)
        west = jnp.where(lane == 0, jnp.broadcast_to(hw[:, l:l + 1], (rows, TLON)), 0.0)
        out_buf[l] = x
        out_buf[l, :, width - TLON:] = x[:, width - TLON:] + wet_right * east
        out_buf[l, :, :TLON] = out_buf[l, :, :TLON] + wet_left * west
        a_row = ha_ref[l:l + 1, :]
        b_row = hb_ref[l:l + 1, :]
        north_row = jnp.where(even, a_row, b_row)
        south_row = jnp.where(even, b_row, a_row)
        out_buf[l, rows - 1:rows, :] = out_buf[l, rows - 1:rows, :] + wet_top * north_row
        out_buf[l, 0:1, :] = out_buf[l, 0:1, :] + wet_bottom * south_row
        copy = pltpu.make_async_copy(out_buf.at[l], out_hbm.at[l], out_sem.at[l])
        copy.start()
        out_copies.append(copy)
        if emit:
            new = out_buf[l]
            coef = (ce[:, l:l + 1], cw[:, l:l + 1], cn_ref[l:l + 1, :], cs_ref[l:l + 1, :], cf_ref[l:l + 1, :])
            out.add(l, *edge_values(*coef, new, rows, width))
    if emit:
        out.finish_pairs(flag_ref, pe_ref, pw_ref, pa_ref, pb_ref)
    for c in out_copies:
        c.wait()


def payload_shapes(levels, rows, width):
    lon = jax.ShapeDtypeStruct((rows, levels), jnp.float32)
    lat = jax.ShapeDtypeStruct((levels, width), jnp.float32)
    return [lon, lon, lat, lat, lat]


def pair_shapes(levels, rows, width):
    return payload_shapes(levels, rows, width)[:4]


def whole(shape):
    return pl.BlockSpec(shape, lambda i, *_: (0,) * len(shape))


def state_spec(k, levels, rows, width):
    return pl.BlockSpec((None, levels, rows, width), lambda i, si, *_: (si[k], 0, 0, 0))


def run_prologue(k, si, wt, flags, af, d, zonal, merid):
    levels, rows, width = af.shape
    shapes = pair_shapes(levels, rows, width)
    anywhere = pl.BlockSpec(memory_space=pl.ANY)
    n = levels * rows * width
    return pl.pallas_call(
        functools.partial(prologue_kernel, k),
        out_shape=shapes,
        grid_spec=pltpu.PrefetchScalarGridSpec(
            num_scalar_prefetch=3,
            grid=(1,),
            in_specs=[anywhere, whole(d.shape), anywhere, anywhere],
            out_specs=[whole(s.shape) for s in shapes],
            scratch_shapes=[pltpu.VMEM(af.shape, jnp.float32) for _ in range(3)]
            + [pltpu.SemaphoreType.DMA((3, levels))],
        ),
        cost_estimate=pl.CostEstimate(flops=2 * n, bytes_accessed=12 * n, transcendentals=0),
    )(si, wt, flags, af, d, zonal, merid)


def run_core(k, k_next, si, wt, lm, adj, d, tracer, zonal, merid):
    levels, rows, width = adj.shape
    first = k_next is not None
    emit = k_next is not None
    state = state_spec(k, levels, rows, width)
    in_specs = [pl.BlockSpec(memory_space=pltpu.SMEM), whole(adj.shape), whole(d.shape), state, state, state]
    args = [si, wt, lm, adj, d, tracer, zonal, merid]
    out_shape = [jax.ShapeDtypeStruct(adj.shape, jnp.float32)]
    if emit:
        nxt = state_spec(k_next, levels, rows, width)
        in_specs += [nxt, nxt]
        args += [zonal, merid]
        out_shape += payload_shapes(levels, rows, width)
    n = levels * rows * width
    outs = pl.pallas_call(
        functools.partial(core_kernel, first, emit),
        out_shape=out_shape,
        grid_spec=pltpu.PrefetchScalarGridSpec(
            num_scalar_prefetch=2,
            grid=(1,),
            in_specs=in_specs,
            out_specs=[whole(s.shape) for s in out_shape],
            scratch_shapes=[pltpu.VMEM((levels, rows, width), jnp.float32)],
        ),
        cost_estimate=pl.CostEstimate(flops=60 * n, bytes_accessed=32 * n, transcendentals=0),
    )(*args)
    return outs[0], outs[1:]


def run_fix(wt, flags, part, halos, coefs):
    levels, rows, width = part.shape
    emit = bool(coefs)
    small = [*halos, *coefs]
    args = [wt, flags, part, *small]
    anywhere = pl.BlockSpec(memory_space=pl.ANY)
    in_specs = [anywhere] + [pl.BlockSpec(memory_space=pltpu.VMEM)] * len(small)
    out_shape = [jax.ShapeDtypeStruct(part.shape, jnp.float32)]
    out_specs = [anywhere]
    if emit:
        shapes = pair_shapes(levels, rows, width)
        out_shape += shapes
        out_specs += [whole(x.shape) for x in shapes]
    scratch = [
        pltpu.VMEM(part.shape, jnp.float32),
        pltpu.VMEM(part.shape, jnp.float32),
        pltpu.SemaphoreType.DMA((levels,)),
        pltpu.SemaphoreType.DMA((levels,)),
    ]
    n = levels * rows * width
    outs = pl.pallas_call(
        functools.partial(fix_kernel, emit, len(small)),
        out_shape=out_shape,
        grid_spec=pltpu.PrefetchScalarGridSpec(
            num_scalar_prefetch=2,
            grid=(1,),
            in_specs=in_specs,
            out_specs=out_specs,
            scratch_shapes=scratch,
        ),
        cost_estimate=pl.CostEstimate(flops=10 * n, bytes_accessed=8 * n, transcendentals=0),
    )(*args)
    return outs[0], outs[1:]


def shards(
    adjoint_final,
    stored_tracer,
    stored_zonal,
    stored_meridional,
    diffusivity,
    level_mixing,
    wet_tiles,
    state_index,
):
    n_lat = lax.axis_size("lat")
    n_lon = lax.axis_size("lon")
    wt = wet_tiles.reshape(-1)
    lat_index = lax.axis_index("lat")
    flags = jnp.stack([lat_index % 2, (lat_index == n_lat - 1).astype(jnp.int32)]).astype(jnp.int32)

    to_west = shift_pairs(n_lon, -1, True)
    to_east = shift_pairs(n_lon, 1, True)
    pairs_a = [(i, i ^ 1) for i in range(n_lat)]
    top = n_lat - 1
    pairs_b = []
    for j in range(n_lon):
        for i in range(1, n_lat - 1, 2):
            pairs_b += [(j * n_lat + i, j * n_lat + i + 1), (j * n_lat + i + 1, j * n_lat + i)]
        pairs_b.append((j * n_lat + top, (n_lon - 1 - j) * n_lat + top))

    def exchange(payloads):
        pe, pw, pa, pb = payloads
        he = lax.ppermute(pe, "lon", to_west)
        hw = lax.ppermute(pw, "lon", to_east)
        ha = lax.ppermute(pa, "lat", pairs_a)
        hb = lax.ppermute(pb, ("lon", "lat"), pairs_b)
        return he, hw, ha, hb

    payloads = run_prologue(STEPS - 1, state_index, wt, flags, adjoint_final, diffusivity,
                            stored_zonal, stored_meridional)
    adj = adjoint_final
    for back in range(STEPS):
        k = STEPS - 1 - back
        k_next = k - 1 if k > 0 else None
        halos = exchange(payloads)
        part, coefs = run_core(k, k_next, state_index, wt, level_mixing, adj, diffusivity,
                               stored_tracer, stored_zonal, stored_meridional)
        adj, payloads = run_fix(wt, flags, part, halos, coefs)
    return adj


def solution(mesh):
    return jax.shard_map(
        shards,
        mesh=mesh,
        in_specs=(
            P(None, "lat", "lon"),
            P(None, None, "lat", "lon"),
            P(None, None, "lat", "lon"),
            P(None, None, "lat", "lon"),
            P("lat", "lon"),
            P(),
            P("lat", "lon"),
            P(),
        ),
        out_specs=P(None, "lat", "lon"),
        check_vma=False,
    )
```

```python
import functools

import jax
import jax.numpy as jnp
from jax import lax
from jax.experimental import pallas as pl
from jax.experimental.pallas import tpu as pltpu
from jax.sharding import PartitionSpec as P

TLON = 128
STEPS = 2


advect_scale = 0.25
damping = 0.3


def shift_pairs(count, delta, periodic):
    pairs = []
    for i in range(count):
        j = i + delta
        if periodic:
            pairs.append((i, j % count))
        elif 0 <= j < count:
            pairs.append((i, j))
    return pairs


def wet_field(wt_ref, rows, width):
    lane = lax.broadcasted_iota(jnp.int32, (rows, width), 1)
    wet_i = jnp.zeros((rows, width), jnp.int32)
    for t in range(width // TLON):
        inside = (lane >= t * TLON) & (lane < (t + 1) * TLON)
        wet_i = jnp.where(inside, wt_ref[t], wet_i)
    return wet_i.astype(jnp.float32)


def reverse_lanes(x):
    width = x.shape[-1]
    i = lax.broadcasted_iota(jnp.int32, (width, width), 0)
    j = lax.broadcasted_iota(jnp.int32, (width, width), 1)
    flip = jnp.where(i + j == width - 1, 1.0, 0.0).astype(jnp.bfloat16)
    x1 = x.astype(jnp.bfloat16)
    r1 = x - x1.astype(jnp.float32)
    x2 = r1.astype(jnp.bfloat16)
    x3 = (r1 - x2.astype(jnp.float32)).astype(jnp.bfloat16)

    def perm(part):
        return jnp.dot(part, flip, preferred_element_type=jnp.float32)

    return (perm(x1) + perm(x2)) + perm(x3)


class Collector:
    def __init__(self, levels, rows, width, reverse_fold):
        self.levels = levels
        self.rows = rows
        self.width = width
        self.reverse_fold = reverse_fold
        self.lane = lax.broadcasted_iota(jnp.int32, (rows, TLON), 1)
        self.row = lax.broadcasted_iota(jnp.int32, (16, width), 0)
        self.cols = [jnp.zeros((rows, TLON), jnp.float32) for _ in range(2)]
        self.rows_acc = [jnp.zeros((16, width), jnp.float32) for _ in range(3)]

    def add(self, l, east, west, north, south, fold):
        for i, col in enumerate((east, west)):
            wide = jnp.broadcast_to(col, (self.rows, TLON))
            self.cols[i] = jnp.where(self.lane == l, wide, self.cols[i])
        for i, line in enumerate((north, south, fold)):
            tall = jnp.broadcast_to(line, (16, self.width))
            self.rows_acc[i] = jnp.where(self.row == l, tall, self.rows_acc[i])

    def finish(self, pe_ref, pw_ref, pn_ref, ps_ref, pf_ref):
        levels = self.levels
        pe_ref[...] = self.cols[0][:, :levels]
        pw_ref[...] = self.cols[1][:, :levels]
        pn_ref[...] = self.rows_acc[0][:levels]
        ps_ref[...] = self.rows_acc[1][:levels]
        fold = self.rows_acc[2]
        if self.reverse_fold:
            fold = reverse_lanes(fold)
        pf_ref[...] = fold[:levels]

    def finish_pairs(self, flag_ref, pe_ref, pw_ref, pa_ref, pb_ref):
        levels = self.levels
        pe_ref[...] = self.cols[0][:, :levels]
        pw_ref[...] = self.cols[1][:, :levels]
        north_going = self.rows_acc[0][:levels]
        south_going = self.rows_acc[1][:levels]
        fold = reverse_lanes(self.rows_acc[2])[:levels]
        even = flag_ref[0] == 0
        top = flag_ref[1] == 1
        pa_ref[...] = jnp.where(even, south_going, north_going)
        pb_ref[...] = jnp.where(top, fold, jnp.where(even, north_going, south_going))


def coefficients(l, d, u, v, rows, width):
    return (
        d[:, 0:1] + advect_scale * u[:, 0:1],
        d[:, width - 1:width] - advect_scale * u[:, width - 1:width],
        d[0:1, :] + advect_scale * v[0:1, :],
        d[rows - 1:rows, :] - advect_scale * v[rows - 1:rows, :],
        d[rows - 1:rows, :] + advect_scale * v[rows - 1:rows, :],
    )


def edge_values(ce, cw, cn, cs, cf, a, rows, width):
    return (
        ce * a[:, 0:1],
        cw * a[:, width - 1:width],
        cn * a[0:1, :],
        cs * a[rows - 1:rows, :],
        cf * a[rows - 1:rows, :],
    )


def prologue_kernel(si_ref, wt_ref, flag_ref, af_ref, d_ref, u_ref, v_ref, pe_ref, pw_ref, pa_ref, pb_ref):
    del si_ref
    levels, rows, width = af_ref.shape
    wet = wet_field(wt_ref, rows, width)
    d = d_ref[...]
    out = Collector(levels, rows, width, True)
    for l in range(levels):
        coef = coefficients(l, d, u_ref[l], v_ref[l], rows, width)
        out.add(l, *edge_values(*coef, af_ref[l] * wet, rows, width))
    out.finish_pairs(flag_ref, pe_ref, pw_ref, pa_ref, pb_ref)


def core_kernel(first, emit, si_ref, wt_ref, lm_ref, adj_ref, d_ref, t_ref, u_ref, v_ref, *rest):
    del si_ref
    if emit:
        u2_ref, v2_ref, out_ref, ce_ref, cw_ref, cn_ref, cs_ref, cf_ref, a_ref = rest
    else:
        out_ref, a_ref = rest
    levels, rows, width = adj_ref.shape
    lane = lax.broadcasted_iota(jnp.int32, (rows, width), 1)
    row = lax.broadcasted_iota(jnp.int32, (rows, width), 0)
    wet = wet_field(wt_ref, rows, width)
    if first:
        for m in range(levels):
            a_ref[m] = adj_ref[m] * wet
        src = a_ref
    else:
        src = adj_ref
    d = d_ref[...]
    coef = Collector(levels, rows, width, False) if emit else None

    for l in range(levels):
        a = src[l]
        vertical = lm_ref[0, l] * src[0]
        for m in range(1, levels):
            vertical = vertical + lm_ref[m, l] * src[m]
        s = d * a
        zf = u_ref[l] * a
        mf = v_ref[l] * a
        east = jnp.where(lane == width - 1, 0.0, pltpu.roll(s + advect_scale * zf, width - 1, 1))
        west = jnp.where(lane == 0, 0.0, pltpu.roll(s - advect_scale * zf, 1, 1))
        north = jnp.where(row == rows - 1, 0.0, pltpu.roll(s + advect_scale * mf, rows - 1, 0))
        south = jnp.where(row == 0, 0.0, pltpu.roll(s - advect_scale * mf, 1, 0))
        t = t_ref[l]
        out_ref[l] = wet * (a - 4.0 * s + east + west + north + south + vertical - damping * t * t * a)
        if emit:
            coef.add(l, *coefficients(l, d, u2_ref[l], v2_ref[l], rows, width))
    if emit:
        coef.finish(ce_ref, cw_ref, cn_ref, cs_ref, cf_ref)


def fix_kernel(emit, wt_ref, flag_ref, part_ref, he_ref, hw_ref, ha_ref, hb_ref, *rest):
    if emit:
        ce_ref, cw_ref, cn_ref, cs_ref, cf_ref, out_ref, pe_ref, pw_ref, pa_ref, pb_ref = rest
    else:
        (out_ref,) = rest
    levels, rows, width = part_ref.shape
    wet = wet_field(wt_ref, rows, width)
    wet_left, wet_right = wet[:, :TLON], wet[:, width - TLON:]
    wet_bottom, wet_top = wet[0:1, :], wet[rows - 1:rows, :]
    lane = lax.broadcasted_iota(jnp.int32, (rows, TLON), 1)
    he = he_ref[...]
    hw = hw_ref[...]
    even = flag_ref[0] == 0
    if emit:
        ce = ce_ref[...]
        cw = cw_ref[...]
        out = Collector(levels, rows, width, True)
    for l in range(levels):
        x = part_ref[l]
        east = jnp.where(lane == TLON - 1, jnp.broadcast_to(he[:, l:l + 1], (rows, TLON)), 0.0)
        west = jnp.where(lane == 0, jnp.broadcast_to(hw[:, l:l + 1], (rows, TLON)), 0.0)
        out_ref[l] = x
        out_ref[l, :, width - TLON:] = x[:, width - TLON:] + wet_right * east
        out_ref[l, :, :TLON] = out_ref[l, :, :TLON] + wet_left * west
        a_row = ha_ref[l:l + 1, :]
        b_row = hb_ref[l:l + 1, :]
        north_row = jnp.where(even, a_row, b_row)
        south_row = jnp.where(even, b_row, a_row)
        out_ref[l, rows - 1:rows, :] = out_ref[l, rows - 1:rows, :] + wet_top * north_row
        out_ref[l, 0:1, :] = out_ref[l, 0:1, :] + wet_bottom * south_row
        if emit:
            new = out_ref[l]
            coef = (ce[:, l:l + 1], cw[:, l:l + 1], cn_ref[l:l + 1, :], cs_ref[l:l + 1, :], cf_ref[l:l + 1, :])
            out.add(l, *edge_values(*coef, new, rows, width))
    if emit:
        out.finish_pairs(flag_ref, pe_ref, pw_ref, pa_ref, pb_ref)


def payload_shapes(levels, rows, width):
    lon = jax.ShapeDtypeStruct((rows, levels), jnp.float32)
    lat = jax.ShapeDtypeStruct((levels, width), jnp.float32)
    return [lon, lon, lat, lat, lat]


def pair_shapes(levels, rows, width):
    return payload_shapes(levels, rows, width)[:4]


def whole(shape):
    return pl.BlockSpec(shape, lambda i, *_: (0,) * len(shape))


def state_spec(k, levels, rows, width):
    return pl.BlockSpec((None, levels, rows, width), lambda i, si, *_: (si[k], 0, 0, 0))


def run_prologue(k, si, wt, flags, af, d, zonal, merid):
    levels, rows, width = af.shape
    shapes = pair_shapes(levels, rows, width)
    n = levels * rows * width
    return pl.pallas_call(
        prologue_kernel,
        out_shape=shapes,
        grid_spec=pltpu.PrefetchScalarGridSpec(
            num_scalar_prefetch=3,
            grid=(1,),
            in_specs=[whole(af.shape), whole(d.shape), state_spec(k, levels, rows, width),
                      state_spec(k, levels, rows, width)],
            out_specs=[whole(s.shape) for s in shapes],
        ),
        cost_estimate=pl.CostEstimate(flops=2 * n, bytes_accessed=12 * n, transcendentals=0),
    )(si, wt, flags, af, d, zonal, merid)


def run_core(k, k_next, si, wt, lm, adj, d, tracer, zonal, merid):
    levels, rows, width = adj.shape
    first = k_next is not None
    emit = k_next is not None
    state = state_spec(k, levels, rows, width)
    in_specs = [pl.BlockSpec(memory_space=pltpu.SMEM), whole(adj.shape), whole(d.shape), state, state, state]
    args = [si, wt, lm, adj, d, tracer, zonal, merid]
    out_shape = [jax.ShapeDtypeStruct(adj.shape, jnp.float32)]
    if emit:
        nxt = state_spec(k_next, levels, rows, width)
        in_specs += [nxt, nxt]
        args += [zonal, merid]
        out_shape += payload_shapes(levels, rows, width)
    n = levels * rows * width
    outs = pl.pallas_call(
        functools.partial(core_kernel, first, emit),
        out_shape=out_shape,
        grid_spec=pltpu.PrefetchScalarGridSpec(
            num_scalar_prefetch=2,
            grid=(1,),
            in_specs=in_specs,
            out_specs=[whole(s.shape) for s in out_shape],
            scratch_shapes=[pltpu.VMEM((levels, rows, width), jnp.float32)],
        ),
        cost_estimate=pl.CostEstimate(flops=60 * n, bytes_accessed=32 * n, transcendentals=0),
    )(*args)
    return outs[0], outs[1:]


def run_fix(wt, flags, part, halos, coefs):
    levels, rows, width = part.shape
    emit = bool(coefs)
    args = [wt, flags, part, *halos, *coefs]
    in_specs = [whole(x.shape) for x in args[2:]]
    out_shape = [jax.ShapeDtypeStruct(part.shape, jnp.float32)]
    if emit:
        out_shape += pair_shapes(levels, rows, width)
    n = levels * rows * width
    outs = pl.pallas_call(
        functools.partial(fix_kernel, emit),
        out_shape=out_shape,
        grid_spec=pltpu.PrefetchScalarGridSpec(
            num_scalar_prefetch=2,
            grid=(1,),
            in_specs=in_specs,
            out_specs=[whole(s.shape) for s in out_shape],
        ),
        cost_estimate=pl.CostEstimate(flops=10 * n, bytes_accessed=8 * n, transcendentals=0),
    )(*args)
    return outs[0], outs[1:]


def fix_in_xla(wet_tiles, lat_index, part, halos):
    levels, rows, width = part.shape
    he, hw, ha, hb = halos
    even = lat_index % 2 == 0
    north = jnp.where(even, ha, hb)
    south = jnp.where(even, hb, ha)
    wet = jnp.repeat(wet_tiles.reshape(-1), TLON).astype(jnp.float32)
    g = lax.broadcasted_iota(jnp.int32, part.shape, 2)
    r = lax.broadcasted_iota(jnp.int32, part.shape, 1)
    corr = (
        jnp.where(g == width - 1, he.T[:, :, None], 0.0)
        + jnp.where(g == 0, hw.T[:, :, None], 0.0)
        + jnp.where(r == rows - 1, north[:, None, :], 0.0)
        + jnp.where(r == 0, south[:, None, :], 0.0)
    )
    return part + wet * corr


def shards(
    adjoint_final,
    stored_tracer,
    stored_zonal,
    stored_meridional,
    diffusivity,
    level_mixing,
    wet_tiles,
    state_index,
):
    n_lat = lax.axis_size("lat")
    n_lon = lax.axis_size("lon")
    wt = wet_tiles.reshape(-1)
    lat_index = lax.axis_index("lat")
    flags = jnp.stack([lat_index % 2, (lat_index == n_lat - 1).astype(jnp.int32)]).astype(jnp.int32)

    to_west = shift_pairs(n_lon, -1, True)
    to_east = shift_pairs(n_lon, 1, True)
    pairs_a = [(i, i ^ 1) for i in range(n_lat)]
    top = n_lat - 1
    pairs_b = []
    for j in range(n_lon):
        for i in range(1, n_lat - 1, 2):
            pairs_b += [(j * n_lat + i, j * n_lat + i + 1), (j * n_lat + i + 1, j * n_lat + i)]
        pairs_b.append((j * n_lat + top, (n_lon - 1 - j) * n_lat + top))

    def exchange(payloads):
        pe, pw, pa, pb = payloads
        he = lax.ppermute(pe, "lon", to_west)
        hw = lax.ppermute(pw, "lon", to_east)
        ha = lax.ppermute(pa, "lat", pairs_a)
        hb = lax.ppermute(pb, ("lon", "lat"), pairs_b)
        return he, hw, ha, hb

    payloads = run_prologue(STEPS - 1, state_index, wt, flags, adjoint_final, diffusivity,
                            stored_zonal, stored_meridional)
    adj = adjoint_final
    for back in range(STEPS):
        k = STEPS - 1 - back
        k_next = k - 1 if k > 0 else None
        halos = exchange(payloads)
        part, coefs = run_core(k, k_next, state_index, wt, level_mixing, adj, diffusivity,
                               stored_tracer, stored_zonal, stored_meridional)
        if coefs:
            adj, payloads = run_fix(wt, flags, part, halos, coefs)
        else:
            adj = fix_in_xla(wet_tiles, lat_index, part, halos)
    return adj


def solution(mesh):
    return jax.shard_map(
        shards,
        mesh=mesh,
        in_specs=(
            P(None, "lat", "lon"),
            P(None, None, "lat", "lon"),
            P(None, None, "lat", "lon"),
            P(None, None, "lat", "lon"),
            P("lat", "lon"),
            P(),
            P("lat", "lon"),
            P(),
        ),
        out_specs=P(None, "lat", "lon"),
        check_vma=False,
    )
```

```python
import functools

import jax
import jax.numpy as jnp
from jax import lax
from jax.experimental import pallas as pl
from jax.experimental.pallas import tpu as pltpu
from jax.sharding import PartitionSpec as P

TLON = 128
STEPS = 2


advect_scale = 0.25
damping = 0.3


def shift_pairs(count, delta, periodic):
    pairs = []
    for i in range(count):
        j = i + delta
        if periodic:
            pairs.append((i, j % count))
        elif 0 <= j < count:
            pairs.append((i, j))
    return pairs


def wet_field(wt_ref, rows, width):
    lane = lax.broadcasted_iota(jnp.int32, (rows, width), 1)
    wet_i = jnp.zeros((rows, width), jnp.int32)
    for t in range(width // TLON):
        inside = (lane >= t * TLON) & (lane < (t + 1) * TLON)
        wet_i = jnp.where(inside, wt_ref[t], wet_i)
    return wet_i.astype(jnp.float32)


def reverse_lanes(x):
    width = x.shape[-1]
    i = lax.broadcasted_iota(jnp.int32, (width, width), 0)
    j = lax.broadcasted_iota(jnp.int32, (width, width), 1)
    flip = jnp.where(i + j == width - 1, 1.0, 0.0).astype(jnp.bfloat16)
    x1 = x.astype(jnp.bfloat16)
    r1 = x - x1.astype(jnp.float32)
    x2 = r1.astype(jnp.bfloat16)
    x3 = (r1 - x2.astype(jnp.float32)).astype(jnp.bfloat16)

    def perm(part):
        return jnp.dot(part, flip, preferred_element_type=jnp.float32)

    return (perm(x1) + perm(x2)) + perm(x3)


class Collector:
    def __init__(self, levels, rows, width, reverse_fold):
        self.levels = levels
        self.rows = rows
        self.width = width
        self.reverse_fold = reverse_fold
        self.lane = lax.broadcasted_iota(jnp.int32, (rows, TLON), 1)
        self.row = lax.broadcasted_iota(jnp.int32, (16, width), 0)
        self.cols = [jnp.zeros((rows, TLON), jnp.float32) for _ in range(2)]
        self.rows_acc = [jnp.zeros((16, width), jnp.float32) for _ in range(3)]

    def add(self, l, east, west, north, south, fold):
        for i, col in enumerate((east, west)):
            wide = jnp.broadcast_to(col, (self.rows, TLON))
            self.cols[i] = jnp.where(self.lane == l, wide, self.cols[i])
        for i, line in enumerate((north, south, fold)):
            tall = jnp.broadcast_to(line, (16, self.width))
            self.rows_acc[i] = jnp.where(self.row == l, tall, self.rows_acc[i])

    def finish(self, pe_ref, pw_ref, pn_ref, ps_ref, pf_ref):
        levels = self.levels
        pe_ref[...] = self.cols[0][:, :levels]
        pw_ref[...] = self.cols[1][:, :levels]
        pn_ref[...] = self.rows_acc[0][:levels]
        ps_ref[...] = self.rows_acc[1][:levels]
        fold = self.rows_acc[2]
        if self.reverse_fold:
            fold = reverse_lanes(fold)
        pf_ref[...] = fold[:levels]

    def finish4(self, ec_ref, wc_ref, sr_ref, nr_ref):
        levels = self.levels
        ec_ref[...] = self.cols[0][:, :levels]
        wc_ref[...] = self.cols[1][:, :levels]
        sr_ref[...] = self.rows_acc[0][:levels]
        nr_ref[...] = self.rows_acc[1][:levels]

    def finish_pairs(self, flag_ref, pe_ref, pw_ref, pa_ref, pb_ref):
        levels = self.levels
        pe_ref[...] = self.cols[0][:, :levels]
        pw_ref[...] = self.cols[1][:, :levels]
        north_going = self.rows_acc[0][:levels]
        south_going = self.rows_acc[1][:levels]
        fold = reverse_lanes(self.rows_acc[2])[:levels]
        even = flag_ref[0] == 0
        top = flag_ref[1] == 1
        pa_ref[...] = jnp.where(even, south_going, north_going)
        pb_ref[...] = jnp.where(top, fold, jnp.where(even, north_going, south_going))


def coefficients(l, d, u, v, rows, width):
    return (
        d[:, 0:1] + advect_scale * u[:, 0:1],
        d[:, width - 1:width] - advect_scale * u[:, width - 1:width],
        d[0:1, :] + advect_scale * v[0:1, :],
        d[rows - 1:rows, :] - advect_scale * v[rows - 1:rows, :],
        d[rows - 1:rows, :] + advect_scale * v[rows - 1:rows, :],
    )


def edge_values(ce, cw, cn, cs, cf, a, rows, width):
    return (
        ce * a[:, 0:1],
        cw * a[:, width - 1:width],
        cn * a[0:1, :],
        cs * a[rows - 1:rows, :],
        cf * a[rows - 1:rows, :],
    )


def prologue_kernel(si_ref, wt_ref, flag_ref, af_ref, d_ref, u_ref, v_ref, pe_ref, pw_ref, pa_ref, pb_ref):
    del si_ref
    levels, rows, width = af_ref.shape
    wet = wet_field(wt_ref, rows, width)
    d = d_ref[...]
    out = Collector(levels, rows, width, True)
    for l in range(levels):
        coef = coefficients(l, d, u_ref[l], v_ref[l], rows, width)
        out.add(l, *edge_values(*coef, af_ref[l] * wet, rows, width))
    out.finish_pairs(flag_ref, pe_ref, pw_ref, pa_ref, pb_ref)


def core_kernel(first, emit, fixin, si_ref, wt_ref, flag_ref, lm_ref, adj_ref, d_ref, t_ref, u_ref, v_ref, *rest):
    del si_ref
    rest = list(rest)
    if fixin:
        he_ref, hw_ref, ha_ref, hb_ref = rest[:4]
        rest = rest[4:]
    if emit:
        u2_ref, v2_ref, out_ref, ce_ref, cw_ref, cn_ref, cs_ref, cf_ref, ec_ref, wc_ref, sr_ref, nr_ref, a_ref = rest
    else:
        out_ref, a_ref = rest
    levels, rows, width = adj_ref.shape
    lane = lax.broadcasted_iota(jnp.int32, (rows, width), 1)
    row = lax.broadcasted_iota(jnp.int32, (rows, width), 0)
    wet = wet_field(wt_ref, rows, width)
    if first:
        for m in range(levels):
            a_ref[m] = adj_ref[m] * wet
        src = a_ref
    elif fixin:
        he = he_ref[...]
        hw = hw_ref[...]
        even = flag_ref[0] == 0
        for m in range(levels):
            a_row = ha_ref[m:m + 1, :]
            b_row = hb_ref[m:m + 1, :]
            corr = (
                jnp.where(lane == width - 1, jnp.broadcast_to(he[:, m:m + 1], (rows, width)), 0.0)
                + jnp.where(lane == 0, jnp.broadcast_to(hw[:, m:m + 1], (rows, width)), 0.0)
                + jnp.where(row == rows - 1, jnp.where(even, a_row, b_row), 0.0)
                + jnp.where(row == 0, jnp.where(even, b_row, a_row), 0.0)
            )
            a_ref[m] = adj_ref[m] + wet * corr
        src = a_ref
    else:
        src = adj_ref
    d = d_ref[...]
    if emit:
        coef = Collector(levels, rows, width, False)
        edges = Collector(levels, rows, width, False)

    for l in range(levels):
        a = src[l]
        vertical = lm_ref[0, l] * src[0]
        for m in range(1, levels):
            vertical = vertical + lm_ref[m, l] * src[m]
        s = d * a
        zf = u_ref[l] * a
        mf = v_ref[l] * a
        east = jnp.where(lane == width - 1, 0.0, pltpu.roll(s + advect_scale * zf, width - 1, 1))
        west = jnp.where(lane == 0, 0.0, pltpu.roll(s - advect_scale * zf, 1, 1))
        north = jnp.where(row == rows - 1, 0.0, pltpu.roll(s + advect_scale * mf, rows - 1, 0))
        south = jnp.where(row == 0, 0.0, pltpu.roll(s - advect_scale * mf, 1, 0))
        t = t_ref[l]
        new = wet * (a - 4.0 * s + east + west + north + south + vertical - damping * t * t * a)
        out_ref[l] = new
        if emit:
            coef.add(l, *coefficients(l, d, u2_ref[l], v2_ref[l], rows, width))
            bottom, top_row = new[0:1, :], new[rows - 1:rows, :]
            edges.add(l, new[:, 0:1], new[:, width - 1:width], bottom, top_row, top_row)
    if emit:
        coef.finish(ce_ref, cw_ref, cn_ref, cs_ref, cf_ref)
        edges.finish4(ec_ref, wc_ref, sr_ref, nr_ref)


def payload_kernel(wt_ref, flag_ref, ec_ref, wc_ref, sr_ref, nr_ref, he_ref, hw_ref, ha_ref, hb_ref,
                   ce_ref, cw_ref, cn_ref, cs_ref, cf_ref, pe_ref, pw_ref, pa_ref, pb_ref):
    rows, levels = ec_ref.shape
    width = sr_ref.shape[1]
    wet_row = wet_field(wt_ref, 1, width)
    wet_first = wet_row[:, 0:1]
    wet_last = wet_row[:, width - 1:width]
    r = lax.broadcasted_iota(jnp.int32, (rows, 1), 0)
    g = lax.broadcasted_iota(jnp.int32, (1, width), 1)
    even = flag_ref[0] == 0
    ec, wc, he, hw, ce, cw = (x[...] for x in (ec_ref, wc_ref, he_ref, hw_ref, ce_ref, cw_ref))
    out = Collector(levels, rows, width, True)
    for l in range(levels):
        a_row = ha_ref[l:l + 1, :]
        b_row = hb_ref[l:l + 1, :]
        north_row = jnp.where(even, a_row, b_row)
        south_row = jnp.where(even, b_row, a_row)
        he_c = he[:, l:l + 1]
        hw_c = hw[:, l:l + 1]
        col_first = ec[:, l:l + 1] + wet_first * (
            hw_c + jnp.where(r == 0, south_row[:, 0:1], 0.0) + jnp.where(r == rows - 1, north_row[:, 0:1], 0.0)
        )
        col_last = wc[:, l:l + 1] + wet_last * (
            he_c
            + jnp.where(r == 0, south_row[:, width - 1:width], 0.0)
            + jnp.where(r == rows - 1, north_row[:, width - 1:width], 0.0)
        )
        row_first = sr_ref[l:l + 1, :] + wet_row * (
            south_row + jnp.where(g == 0, hw_c[0:1, :], 0.0) + jnp.where(g == width - 1, he_c[0:1, :], 0.0)
        )
        row_last = nr_ref[l:l + 1, :] + wet_row * (
            north_row
            + jnp.where(g == 0, hw_c[rows - 1:rows, :], 0.0)
            + jnp.where(g == width - 1, he_c[rows - 1:rows, :], 0.0)
        )
        out.add(
            l,
            ce[:, l:l + 1] * col_first,
            cw[:, l:l + 1] * col_last,
            cn_ref[l:l + 1, :] * row_first,
            cs_ref[l:l + 1, :] * row_last,
            cf_ref[l:l + 1, :] * row_last,
        )
    out.finish_pairs(flag_ref, pe_ref, pw_ref, pa_ref, pb_ref)


def fix_kernel(emit, wt_ref, flag_ref, part_ref, he_ref, hw_ref, ha_ref, hb_ref, *rest):
    if emit:
        ce_ref, cw_ref, cn_ref, cs_ref, cf_ref, out_ref, pe_ref, pw_ref, pa_ref, pb_ref = rest
    else:
        (out_ref,) = rest
    levels, rows, width = part_ref.shape
    wet = wet_field(wt_ref, rows, width)
    wet_left, wet_right = wet[:, :TLON], wet[:, width - TLON:]
    wet_bottom, wet_top = wet[0:1, :], wet[rows - 1:rows, :]
    lane = lax.broadcasted_iota(jnp.int32, (rows, TLON), 1)
    he = he_ref[...]
    hw = hw_ref[...]
    even = flag_ref[0] == 0
    if emit:
        ce = ce_ref[...]
        cw = cw_ref[...]
        out = Collector(levels, rows, width, True)
    for l in range(levels):
        x = part_ref[l]
        east = jnp.where(lane == TLON - 1, jnp.broadcast_to(he[:, l:l + 1], (rows, TLON)), 0.0)
        west = jnp.where(lane == 0, jnp.broadcast_to(hw[:, l:l + 1], (rows, TLON)), 0.0)
        out_ref[l] = x
        out_ref[l, :, width - TLON:] = x[:, width - TLON:] + wet_right * east
        out_ref[l, :, :TLON] = out_ref[l, :, :TLON] + wet_left * west
        a_row = ha_ref[l:l + 1, :]
        b_row = hb_ref[l:l + 1, :]
        north_row = jnp.where(even, a_row, b_row)
        south_row = jnp.where(even, b_row, a_row)
        out_ref[l, rows - 1:rows, :] = out_ref[l, rows - 1:rows, :] + wet_top * north_row
        out_ref[l, 0:1, :] = out_ref[l, 0:1, :] + wet_bottom * south_row
        if emit:
            new = out_ref[l]
            coef = (ce[:, l:l + 1], cw[:, l:l + 1], cn_ref[l:l + 1, :], cs_ref[l:l + 1, :], cf_ref[l:l + 1, :])
            out.add(l, *edge_values(*coef, new, rows, width))
    if emit:
        out.finish_pairs(flag_ref, pe_ref, pw_ref, pa_ref, pb_ref)


def payload_shapes(levels, rows, width):
    lon = jax.ShapeDtypeStruct((rows, levels), jnp.float32)
    lat = jax.ShapeDtypeStruct((levels, width), jnp.float32)
    return [lon, lon, lat, lat, lat]


def pair_shapes(levels, rows, width):
    return payload_shapes(levels, rows, width)[:4]


def whole(shape):
    return pl.BlockSpec(shape, lambda i, *_: (0,) * len(shape))


def state_spec(k, levels, rows, width):
    return pl.BlockSpec((None, levels, rows, width), lambda i, si, *_: (si[k], 0, 0, 0))


def run_prologue(k, si, wt, flags, af, d, zonal, merid):
    levels, rows, width = af.shape
    shapes = pair_shapes(levels, rows, width)
    n = levels * rows * width
    return pl.pallas_call(
        prologue_kernel,
        out_shape=shapes,
        grid_spec=pltpu.PrefetchScalarGridSpec(
            num_scalar_prefetch=3,
            grid=(1,),
            in_specs=[whole(af.shape), whole(d.shape), state_spec(k, levels, rows, width),
                      state_spec(k, levels, rows, width)],
            out_specs=[whole(s.shape) for s in shapes],
        ),
        cost_estimate=pl.CostEstimate(flops=2 * n, bytes_accessed=12 * n, transcendentals=0),
    )(si, wt, flags, af, d, zonal, merid)


def run_core(k, k_next, si, wt, flags, lm, adj, d, tracer, zonal, merid, halos=()):
    levels, rows, width = adj.shape
    first = k_next is not None
    emit = k_next is not None
    fixin = bool(halos)
    state = state_spec(k, levels, rows, width)
    in_specs = [pl.BlockSpec(memory_space=pltpu.SMEM), whole(adj.shape), whole(d.shape), state, state, state]
    args = [si, wt, flags, lm, adj, d, tracer, zonal, merid]
    if fixin:
        in_specs += [whole(h.shape) for h in halos]
        args += list(halos)
    out_shape = [jax.ShapeDtypeStruct(adj.shape, jnp.float32)]
    if emit:
        nxt = state_spec(k_next, levels, rows, width)
        in_specs += [nxt, nxt]
        args += [zonal, merid]
        out_shape += payload_shapes(levels, rows, width) + pair_shapes(levels, rows, width)
    n = levels * rows * width
    outs = pl.pallas_call(
        functools.partial(core_kernel, first, emit, fixin),
        out_shape=out_shape,
        grid_spec=pltpu.PrefetchScalarGridSpec(
            num_scalar_prefetch=3,
            grid=(1,),
            in_specs=in_specs,
            out_specs=[whole(s.shape) for s in out_shape],
            scratch_shapes=[pltpu.VMEM((levels, rows, width), jnp.float32)],
        ),
        cost_estimate=pl.CostEstimate(flops=60 * n, bytes_accessed=32 * n, transcendentals=0),
    )(*args)
    return outs[0], outs[1:6], outs[6:]


def run_payload(wt, flags, edges, halos, coefs):
    small = [*edges, *halos, *coefs]
    rows, levels = edges[0].shape
    width = edges[2].shape[1]
    shapes = pair_shapes(levels, rows, width)
    return pl.pallas_call(
        payload_kernel,
        out_shape=shapes,
        grid_spec=pltpu.PrefetchScalarGridSpec(
            num_scalar_prefetch=2,
            grid=(1,),
            in_specs=[whole(x.shape) for x in small],
            out_specs=[whole(x.shape) for x in shapes],
        ),
        cost_estimate=pl.CostEstimate(flops=40 * levels * width, bytes_accessed=64 * levels * width,
                                      transcendentals=0),
    )(wt, flags, *small)


def run_fix(wt, flags, part, halos, coefs):
    levels, rows, width = part.shape
    emit = bool(coefs)
    args = [wt, flags, part, *halos, *coefs]
    in_specs = [whole(x.shape) for x in args[2:]]
    out_shape = [jax.ShapeDtypeStruct(part.shape, jnp.float32)]
    if emit:
        out_shape += pair_shapes(levels, rows, width)
    n = levels * rows * width
    outs = pl.pallas_call(
        functools.partial(fix_kernel, emit),
        out_shape=out_shape,
        grid_spec=pltpu.PrefetchScalarGridSpec(
            num_scalar_prefetch=2,
            grid=(1,),
            in_specs=in_specs,
            out_specs=[whole(s.shape) for s in out_shape],
        ),
        cost_estimate=pl.CostEstimate(flops=10 * n, bytes_accessed=8 * n, transcendentals=0),
    )(*args)
    return outs[0], outs[1:]


def fix_in_xla(wet_tiles, lat_index, part, halos):
    levels, rows, width = part.shape
    he, hw, ha, hb = halos
    even = lat_index % 2 == 0
    north = jnp.where(even, ha, hb)
    south = jnp.where(even, hb, ha)
    wet = jnp.repeat(wet_tiles.reshape(-1), TLON).astype(jnp.float32)
    g = lax.broadcasted_iota(jnp.int32, part.shape, 2)
    r = lax.broadcasted_iota(jnp.int32, part.shape, 1)
    corr = (
        jnp.where(g == width - 1, he.T[:, :, None], 0.0)
        + jnp.where(g == 0, hw.T[:, :, None], 0.0)
        + jnp.where(r == rows - 1, north[:, None, :], 0.0)
        + jnp.where(r == 0, south[:, None, :], 0.0)
    )
    return part + wet * corr


def shards(
    adjoint_final,
    stored_tracer,
    stored_zonal,
    stored_meridional,
    diffusivity,
    level_mixing,
    wet_tiles,
    state_index,
):
    n_lat = lax.axis_size("lat")
    n_lon = lax.axis_size("lon")
    wt = wet_tiles.reshape(-1)
    lat_index = lax.axis_index("lat")
    flags = jnp.stack([lat_index % 2, (lat_index == n_lat - 1).astype(jnp.int32)]).astype(jnp.int32)

    to_west = shift_pairs(n_lon, -1, True)
    to_east = shift_pairs(n_lon, 1, True)
    pairs_a = [(i, i ^ 1) for i in range(n_lat)]
    top = n_lat - 1
    pairs_b = []
    for j in range(n_lon):
        for i in range(1, n_lat - 1, 2):
            pairs_b += [(j * n_lat + i, j * n_lat + i + 1), (j * n_lat + i + 1, j * n_lat + i)]
        pairs_b.append((j * n_lat + top, (n_lon - 1 - j) * n_lat + top))

    def exchange(payloads):
        pe, pw, pa, pb = payloads
        he = lax.ppermute(pe, "lon", to_west)
        hw = lax.ppermute(pw, "lon", to_east)
        ha = lax.ppermute(pa, "lat", pairs_a)
        hb = lax.ppermute(pb, ("lon", "lat"), pairs_b)
        return he, hw, ha, hb

    payloads = run_prologue(STEPS - 1, state_index, wt, flags, adjoint_final, diffusivity,
                            stored_zonal, stored_meridional)
    adj = adjoint_final
    previous = ()
    for back in range(STEPS):
        k = STEPS - 1 - back
        k_next = k - 1 if k > 0 else None
        halos = exchange(payloads)
        part, coefs, edges = run_core(k, k_next, state_index, wt, flags, level_mixing, adj, diffusivity,
                                      stored_tracer, stored_zonal, stored_meridional, previous)
        if coefs:
            payloads = run_payload(wt, flags, edges, halos, coefs)
            adj = part
            previous = halos
        else:
            adj = fix_in_xla(wet_tiles, lat_index, part, halos)
    return adj


def solution(mesh):
    return jax.shard_map(
        shards,
        mesh=mesh,
        in_specs=(
            P(None, "lat", "lon"),
            P(None, None, "lat", "lon"),
            P(None, None, "lat", "lon"),
            P(None, None, "lat", "lon"),
            P("lat", "lon"),
            P(),
            P("lat", "lon"),
            P(),
        ),
        out_specs=P(None, "lat", "lon"),
        check_vma=False,
    )
```

```python
import functools

import jax
import jax.numpy as jnp
from jax import lax
from jax.experimental import pallas as pl
from jax.experimental.pallas import tpu as pltpu
from jax.sharding import PartitionSpec as P

TLON = 128
STEPS = 2


advect_scale = 0.25
damping = 0.3


def shift_pairs(count, delta, periodic):
    pairs = []
    for i in range(count):
        j = i + delta
        if periodic:
            pairs.append((i, j % count))
        elif 0 <= j < count:
            pairs.append((i, j))
    return pairs


def wet_field(wt_ref, rows, width):
    lane = lax.broadcasted_iota(jnp.int32, (rows, width), 1)
    wet_i = jnp.zeros((rows, width), jnp.int32)
    for t in range(width // TLON):
        inside = (lane >= t * TLON) & (lane < (t + 1) * TLON)
        wet_i = jnp.where(inside, wt_ref[t], wet_i)
    return wet_i.astype(jnp.float32)


def reverse_lanes(x):
    width = x.shape[-1]
    i = lax.broadcasted_iota(jnp.int32, (width, width), 0)
    j = lax.broadcasted_iota(jnp.int32, (width, width), 1)
    flip = jnp.where(i + j == width - 1, 1.0, 0.0).astype(jnp.bfloat16)
    x1 = x.astype(jnp.bfloat16)
    r1 = x - x1.astype(jnp.float32)
    x2 = r1.astype(jnp.bfloat16)
    x3 = (r1 - x2.astype(jnp.float32)).astype(jnp.bfloat16)

    def perm(part):
        return jnp.dot(part, flip, preferred_element_type=jnp.float32)

    return (perm(x1) + perm(x2)) + perm(x3)


class Collector:
    def __init__(self, levels, rows, width, reverse_fold):
        self.levels = levels
        self.rows = rows
        self.width = width
        self.reverse_fold = reverse_fold
        self.lane = lax.broadcasted_iota(jnp.int32, (rows, TLON), 1)
        self.row = lax.broadcasted_iota(jnp.int32, (16, width), 0)
        self.cols = [jnp.zeros((rows, TLON), jnp.float32) for _ in range(2)]
        self.rows_acc = [jnp.zeros((16, width), jnp.float32) for _ in range(3)]

    def add(self, l, east, west, north, south, fold):
        for i, col in enumerate((east, west)):
            wide = jnp.broadcast_to(col, (self.rows, TLON))
            self.cols[i] = jnp.where(self.lane == l, wide, self.cols[i])
        for i, line in enumerate((north, south, fold)):
            tall = jnp.broadcast_to(line, (16, self.width))
            self.rows_acc[i] = jnp.where(self.row == l, tall, self.rows_acc[i])

    def finish(self, pe_ref, pw_ref, pn_ref, ps_ref, pf_ref):
        levels = self.levels
        pe_ref[...] = self.cols[0][:, :levels]
        pw_ref[...] = self.cols[1][:, :levels]
        pn_ref[...] = self.rows_acc[0][:levels]
        ps_ref[...] = self.rows_acc[1][:levels]
        fold = self.rows_acc[2]
        if self.reverse_fold:
            fold = reverse_lanes(fold)
        pf_ref[...] = fold[:levels]

    def finish4(self, ec_ref, wc_ref, sr_ref, nr_ref):
        levels = self.levels
        ec_ref[...] = self.cols[0][:, :levels]
        wc_ref[...] = self.cols[1][:, :levels]
        sr_ref[...] = self.rows_acc[0][:levels]
        nr_ref[...] = self.rows_acc[1][:levels]

    def finish_pairs(self, flag_ref, pe_ref, pw_ref, pa_ref, pb_ref):
        levels = self.levels
        pe_ref[...] = self.cols[0][:, :levels]
        pw_ref[...] = self.cols[1][:, :levels]
        north_going = self.rows_acc[0][:levels]
        south_going = self.rows_acc[1][:levels]
        fold = reverse_lanes(self.rows_acc[2])[:levels]
        even = flag_ref[0] == 0
        top = flag_ref[1] == 1
        pa_ref[...] = jnp.where(even, south_going, north_going)
        pb_ref[...] = jnp.where(top, fold, jnp.where(even, north_going, south_going))


def coefficients(l, d, u, v, rows, width):
    return (
        d[:, 0:1] + advect_scale * u[:, 0:1],
        d[:, width - 1:width] - advect_scale * u[:, width - 1:width],
        d[0:1, :] + advect_scale * v[0:1, :],
        d[rows - 1:rows, :] - advect_scale * v[rows - 1:rows, :],
        d[rows - 1:rows, :] + advect_scale * v[rows - 1:rows, :],
    )


def edge_values(ce, cw, cn, cs, cf, a, rows, width):
    return (
        ce * a[:, 0:1],
        cw * a[:, width - 1:width],
        cn * a[0:1, :],
        cs * a[rows - 1:rows, :],
        cf * a[rows - 1:rows, :],
    )


def prologue_kernel(si_ref, wt_ref, flag_ref, af_ref, d_ref, u_ref, v_ref, pe_ref, pw_ref, pa_ref, pb_ref):
    del si_ref
    levels, rows, width = af_ref.shape
    wet = wet_field(wt_ref, rows, width)
    d = d_ref[...]
    out = Collector(levels, rows, width, True)
    for l in range(levels):
        coef = coefficients(l, d, u_ref[l], v_ref[l], rows, width)
        out.add(l, *edge_values(*coef, af_ref[l] * wet, rows, width))
    out.finish_pairs(flag_ref, pe_ref, pw_ref, pa_ref, pb_ref)


def core_kernel(first, emit, fixin, si_ref, wt_ref, flag_ref, lm_ref, adj_ref, d_ref, t_ref, u_ref, v_ref, *rest):
    del si_ref
    rest = list(rest)
    if fixin:
        he_ref, hw_ref, ha_ref, hb_ref = rest[:4]
        rest = rest[4:]
    if emit:
        u2_ref, v2_ref, out_ref, lon_ref, lat_ref, a_ref = rest
    else:
        out_ref, a_ref = rest
    levels, rows, width = adj_ref.shape
    lane = lax.broadcasted_iota(jnp.int32, (rows, width), 1)
    row = lax.broadcasted_iota(jnp.int32, (rows, width), 0)
    wet = wet_field(wt_ref, rows, width)
    if first:
        for m in range(levels):
            a_ref[m] = adj_ref[m] * wet
        src = a_ref
    elif fixin:
        he = he_ref[...]
        hw = hw_ref[...]
        even = flag_ref[0] == 0
        for m in range(levels):
            a_row = ha_ref[m:m + 1, :]
            b_row = hb_ref[m:m + 1, :]
            corr = (
                jnp.where(lane == width - 1, jnp.broadcast_to(he[:, m:m + 1], (rows, width)), 0.0)
                + jnp.where(lane == 0, jnp.broadcast_to(hw[:, m:m + 1], (rows, width)), 0.0)
                + jnp.where(row == rows - 1, jnp.where(even, a_row, b_row), 0.0)
                + jnp.where(row == 0, jnp.where(even, b_row, a_row), 0.0)
            )
            a_ref[m] = adj_ref[m] + wet * corr
        src = a_ref
    else:
        src = adj_ref
    d = d_ref[...]
    if emit:
        lon_lane = lax.broadcasted_iota(jnp.int32, (rows, TLON), 1)
        lat_rows = -(-5 * levels // 8) * 8
        lat_row = lax.broadcasted_iota(jnp.int32, (lat_rows, width), 0)
        lon_acc = jnp.zeros((rows, TLON), jnp.float32)
        lat_acc = jnp.zeros((lat_rows, width), jnp.float32)

    for l in range(levels):
        a = src[l]
        vertical = lm_ref[0, l] * src[0]
        for m in range(1, levels):
            vertical = vertical + lm_ref[m, l] * src[m]
        s = d * a
        zf = u_ref[l] * a
        mf = v_ref[l] * a
        east = jnp.where(lane == width - 1, 0.0, pltpu.roll(s + advect_scale * zf, width - 1, 1))
        west = jnp.where(lane == 0, 0.0, pltpu.roll(s - advect_scale * zf, 1, 1))
        north = jnp.where(row == rows - 1, 0.0, pltpu.roll(s + advect_scale * mf, rows - 1, 0))
        south = jnp.where(row == 0, 0.0, pltpu.roll(s - advect_scale * mf, 1, 0))
        t = t_ref[l]
        new = wet * (a - 4.0 * s + east + west + north + south + vertical - damping * t * t * a)
        out_ref[l] = new
        if emit:
            ce, cw, cn, cs, cf = coefficients(l, d, u2_ref[l], v2_ref[l], rows, width)
            for j, col in enumerate((ce, cw, new[:, 0:1], new[:, width - 1:width])):
                lon_acc = jnp.where(lon_lane == j * levels + l, jnp.broadcast_to(col, (rows, TLON)), lon_acc)
            for j, line in enumerate((cn, cs, cf, new[0:1, :], new[rows - 1:rows, :])):
                lat_acc = jnp.where(lat_row == j * levels + l, jnp.broadcast_to(line, lat_acc.shape), lat_acc)
    if emit:
        lon_ref[...] = lon_acc[:, : 4 * levels]
        lat_ref[...] = lat_acc[: 5 * levels]


def payload_kernel(wt_ref, flag_ref, lon_ref, lat_ref, he_ref, hw_ref, ha_ref, hb_ref, pe_ref, pw_ref, pa_ref, pb_ref):
    rows, levels = he_ref.shape
    width = ha_ref.shape[1]
    wet_row = wet_field(wt_ref, 1, width)
    wet_first = wet_row[:, 0:1]
    wet_last = wet_row[:, width - 1:width]
    r = lax.broadcasted_iota(jnp.int32, (rows, 1), 0)
    g = lax.broadcasted_iota(jnp.int32, (1, width), 1)
    even = flag_ref[0] == 0
    lon, he, hw = lon_ref[...], he_ref[...], hw_ref[...]
    ce, cw, ec, wc = (lon[:, j * levels:(j + 1) * levels] for j in range(4))

    def lat(j, l):
        return lat_ref[j * levels + l:j * levels + l + 1, :]

    out = Collector(levels, rows, width, True)
    for l in range(levels):
        a_row = ha_ref[l:l + 1, :]
        b_row = hb_ref[l:l + 1, :]
        north_row = jnp.where(even, a_row, b_row)
        south_row = jnp.where(even, b_row, a_row)
        he_c = he[:, l:l + 1]
        hw_c = hw[:, l:l + 1]
        col_first = ec[:, l:l + 1] + wet_first * (
            hw_c + jnp.where(r == 0, south_row[:, 0:1], 0.0) + jnp.where(r == rows - 1, north_row[:, 0:1], 0.0)
        )
        col_last = wc[:, l:l + 1] + wet_last * (
            he_c
            + jnp.where(r == 0, south_row[:, width - 1:width], 0.0)
            + jnp.where(r == rows - 1, north_row[:, width - 1:width], 0.0)
        )
        row_first = lat(3, l) + wet_row * (
            south_row + jnp.where(g == 0, hw_c[0:1, :], 0.0) + jnp.where(g == width - 1, he_c[0:1, :], 0.0)
        )
        row_last = lat(4, l) + wet_row * (
            north_row
            + jnp.where(g == 0, hw_c[rows - 1:rows, :], 0.0)
            + jnp.where(g == width - 1, he_c[rows - 1:rows, :], 0.0)
        )
        out.add(
            l,
            ce[:, l:l + 1] * col_first,
            cw[:, l:l + 1] * col_last,
            lat(0, l) * row_first,
            lat(1, l) * row_last,
            lat(2, l) * row_last,
        )
    out.finish_pairs(flag_ref, pe_ref, pw_ref, pa_ref, pb_ref)


def fix_kernel(emit, wt_ref, flag_ref, part_ref, he_ref, hw_ref, ha_ref, hb_ref, *rest):
    if emit:
        ce_ref, cw_ref, cn_ref, cs_ref, cf_ref, out_ref, pe_ref, pw_ref, pa_ref, pb_ref = rest
    else:
        (out_ref,) = rest
    levels, rows, width = part_ref.shape
    wet = wet_field(wt_ref, rows, width)
    wet_left, wet_right = wet[:, :TLON], wet[:, width - TLON:]
    wet_bottom, wet_top = wet[0:1, :], wet[rows - 1:rows, :]
    lane = lax.broadcasted_iota(jnp.int32, (rows, TLON), 1)
    he = he_ref[...]
    hw = hw_ref[...]
    even = flag_ref[0] == 0
    if emit:
        ce = ce_ref[...]
        cw = cw_ref[...]
        out = Collector(levels, rows, width, True)
    for l in range(levels):
        x = part_ref[l]
        east = jnp.where(lane == TLON - 1, jnp.broadcast_to(he[:, l:l + 1], (rows, TLON)), 0.0)
        west = jnp.where(lane == 0, jnp.broadcast_to(hw[:, l:l + 1], (rows, TLON)), 0.0)
        out_ref[l] = x
        out_ref[l, :, width - TLON:] = x[:, width - TLON:] + wet_right * east
        out_ref[l, :, :TLON] = out_ref[l, :, :TLON] + wet_left * west
        a_row = ha_ref[l:l + 1, :]
        b_row = hb_ref[l:l + 1, :]
        north_row = jnp.where(even, a_row, b_row)
        south_row = jnp.where(even, b_row, a_row)
        out_ref[l, rows - 1:rows, :] = out_ref[l, rows - 1:rows, :] + wet_top * north_row
        out_ref[l, 0:1, :] = out_ref[l, 0:1, :] + wet_bottom * south_row
        if emit:
            new = out_ref[l]
            coef = (ce[:, l:l + 1], cw[:, l:l + 1], cn_ref[l:l + 1, :], cs_ref[l:l + 1, :], cf_ref[l:l + 1, :])
            out.add(l, *edge_values(*coef, new, rows, width))
    if emit:
        out.finish_pairs(flag_ref, pe_ref, pw_ref, pa_ref, pb_ref)


def payload_shapes(levels, rows, width):
    lon = jax.ShapeDtypeStruct((rows, levels), jnp.float32)
    lat = jax.ShapeDtypeStruct((levels, width), jnp.float32)
    return [lon, lon, lat, lat, lat]


def pair_shapes(levels, rows, width):
    return payload_shapes(levels, rows, width)[:4]


def whole(shape):
    return pl.BlockSpec(shape, lambda i, *_: (0,) * len(shape))


def state_spec(k, levels, rows, width):
    return pl.BlockSpec((None, levels, rows, width), lambda i, si, *_: (si[k], 0, 0, 0))


def run_prologue(k, si, wt, flags, af, d, zonal, merid):
    levels, rows, width = af.shape
    shapes = pair_shapes(levels, rows, width)
    n = levels * rows * width
    return pl.pallas_call(
        prologue_kernel,
        out_shape=shapes,
        grid_spec=pltpu.PrefetchScalarGridSpec(
            num_scalar_prefetch=3,
            grid=(1,),
            in_specs=[whole(af.shape), whole(d.shape), state_spec(k, levels, rows, width),
                      state_spec(k, levels, rows, width)],
            out_specs=[whole(s.shape) for s in shapes],
        ),
        cost_estimate=pl.CostEstimate(flops=2 * n, bytes_accessed=12 * n, transcendentals=0),
    )(si, wt, flags, af, d, zonal, merid)


def run_core(k, k_next, si, wt, flags, lm, adj, d, tracer, zonal, merid, halos=()):
    levels, rows, width = adj.shape
    first = k_next is not None
    emit = k_next is not None
    fixin = bool(halos)
    state = state_spec(k, levels, rows, width)
    in_specs = [pl.BlockSpec(memory_space=pltpu.SMEM), whole(adj.shape), whole(d.shape), state, state, state]
    args = [si, wt, flags, lm, adj, d, tracer, zonal, merid]
    if fixin:
        in_specs += [whole(h.shape) for h in halos]
        args += list(halos)
    out_shape = [jax.ShapeDtypeStruct(adj.shape, jnp.float32)]
    if emit:
        nxt = state_spec(k_next, levels, rows, width)
        in_specs += [nxt, nxt]
        args += [zonal, merid]
        out_shape += [jax.ShapeDtypeStruct((rows, 4 * levels), jnp.float32),
                      jax.ShapeDtypeStruct((5 * levels, width), jnp.float32)]
    n = levels * rows * width
    outs = pl.pallas_call(
        functools.partial(core_kernel, first, emit, fixin),
        out_shape=out_shape,
        grid_spec=pltpu.PrefetchScalarGridSpec(
            num_scalar_prefetch=3,
            grid=(1,),
            in_specs=in_specs,
            out_specs=[whole(s.shape) for s in out_shape],
            scratch_shapes=[pltpu.VMEM((levels, rows, width), jnp.float32)],
        ),
        cost_estimate=pl.CostEstimate(flops=60 * n, bytes_accessed=32 * n, transcendentals=0),
    )(*args)
    return outs[0], outs[1:]


def run_payload(wt, flags, packed, halos):
    small = [*packed, *halos]
    rows, levels = halos[0].shape
    width = halos[2].shape[1]
    shapes = pair_shapes(levels, rows, width)
    return pl.pallas_call(
        payload_kernel,
        out_shape=shapes,
        grid_spec=pltpu.PrefetchScalarGridSpec(
            num_scalar_prefetch=2,
            grid=(1,),
            in_specs=[whole(x.shape) for x in small],
            out_specs=[whole(x.shape) for x in shapes],
        ),
        cost_estimate=pl.CostEstimate(flops=40 * levels * width, bytes_accessed=64 * levels * width,
                                      transcendentals=0),
    )(wt, flags, *small)


def fix_in_xla(wet_tiles, lat_index, part, halos):
    levels, rows, width = part.shape
    he, hw, ha, hb = halos
    even = lat_index % 2 == 0
    north = jnp.where(even, ha, hb)
    south = jnp.where(even, hb, ha)
    wet = jnp.repeat(wet_tiles.reshape(-1), TLON).astype(jnp.float32)
    g = lax.broadcasted_iota(jnp.int32, part.shape, 2)
    r = lax.broadcasted_iota(jnp.int32, part.shape, 1)
    corr = (
        jnp.where(g == width - 1, he.T[:, :, None], 0.0)
        + jnp.where(g == 0, hw.T[:, :, None], 0.0)
        + jnp.where(r == rows - 1, north[:, None, :], 0.0)
        + jnp.where(r == 0, south[:, None, :], 0.0)
    )
    return part + wet * corr


def shards(
    adjoint_final,
    stored_tracer,
    stored_zonal,
    stored_meridional,
    diffusivity,
    level_mixing,
    wet_tiles,
    state_index,
):
    n_lat = lax.axis_size("lat")
    n_lon = lax.axis_size("lon")
    wt = wet_tiles.reshape(-1)
    lat_index = lax.axis_index("lat")
    flags = jnp.stack([lat_index % 2, (lat_index == n_lat - 1).astype(jnp.int32)]).astype(jnp.int32)

    to_west = shift_pairs(n_lon, -1, True)
    to_east = shift_pairs(n_lon, 1, True)
    pairs_a = [(i, i ^ 1) for i in range(n_lat)]
    top = n_lat - 1
    pairs_b = []
    for j in range(n_lon):
        for i in range(1, n_lat - 1, 2):
            pairs_b += [(j * n_lat + i, j * n_lat + i + 1), (j * n_lat + i + 1, j * n_lat + i)]
        pairs_b.append((j * n_lat + top, (n_lon - 1 - j) * n_lat + top))

    def exchange(payloads):
        pe, pw, pa, pb = payloads
        he = lax.ppermute(pe, "lon", to_west)
        hw = lax.ppermute(pw, "lon", to_east)
        ha = lax.ppermute(pa, "lat", pairs_a)
        hb = lax.ppermute(pb, ("lon", "lat"), pairs_b)
        return he, hw, ha, hb

    payloads = run_prologue(STEPS - 1, state_index, wt, flags, adjoint_final, diffusivity,
                            stored_zonal, stored_meridional)
    adj = adjoint_final
    previous = ()
    for back in range(STEPS):
        k = STEPS - 1 - back
        k_next = k - 1 if k > 0 else None
        halos = exchange(payloads)
        part, packed = run_core(k, k_next, state_index, wt, flags, level_mixing, adj, diffusivity,
                                stored_tracer, stored_zonal, stored_meridional, previous)
        if packed:
            payloads = run_payload(wt, flags, packed, halos)
            adj = part
            previous = halos
        else:
            adj = fix_in_xla(wet_tiles, lat_index, part, halos)
    return adj


def solution(mesh):
    return jax.shard_map(
        shards,
        mesh=mesh,
        in_specs=(
            P(None, "lat", "lon"),
            P(None, None, "lat", "lon"),
            P(None, None, "lat", "lon"),
            P(None, None, "lat", "lon"),
            P("lat", "lon"),
            P(),
            P("lat", "lon"),
            P(),
        ),
        out_specs=P(None, "lat", "lon"),
        check_vma=False,
    )
```

```python
import functools

import jax
import jax.numpy as jnp
from jax import lax
from jax.experimental import pallas as pl
from jax.experimental.pallas import tpu as pltpu
from jax.sharding import PartitionSpec as P

TLON = 128
STEPS = 2


advect_scale = 0.25
damping = 0.3


def shift_pairs(count, delta, periodic):
    pairs = []
    for i in range(count):
        j = i + delta
        if periodic:
            pairs.append((i, j % count))
        elif 0 <= j < count:
            pairs.append((i, j))
    return pairs


def wet_field(wt_ref, rows, width):
    lane = lax.broadcasted_iota(jnp.int32, (rows, width), 1)
    wet_i = jnp.zeros((rows, width), jnp.int32)
    for t in range(width // TLON):
        inside = (lane >= t * TLON) & (lane < (t + 1) * TLON)
        wet_i = jnp.where(inside, wt_ref[t], wet_i)
    return wet_i.astype(jnp.float32)


def reverse_lanes(x):
    width = x.shape[-1]
    i = lax.broadcasted_iota(jnp.int32, (width, width), 0)
    j = lax.broadcasted_iota(jnp.int32, (width, width), 1)
    flip = jnp.where(i + j == width - 1, 1.0, 0.0).astype(jnp.bfloat16)
    x1 = x.astype(jnp.bfloat16)
    r1 = x - x1.astype(jnp.float32)
    x2 = r1.astype(jnp.bfloat16)
    x3 = (r1 - x2.astype(jnp.float32)).astype(jnp.bfloat16)

    def perm(part):
        return jnp.dot(part, flip, preferred_element_type=jnp.float32)

    return (perm(x1) + perm(x2)) + perm(x3)


def lat_position(n_lat):
    lat = lax.axis_index("lat")
    return lat % 2 == 0, lat == n_lat - 1


class Collector:
    def __init__(self, levels, rows, width, reverse_fold):
        self.levels = levels
        self.rows = rows
        self.width = width
        self.reverse_fold = reverse_fold
        self.lane = lax.broadcasted_iota(jnp.int32, (rows, TLON), 1)
        self.row = lax.broadcasted_iota(jnp.int32, (16, width), 0)
        self.cols = [jnp.zeros((rows, TLON), jnp.float32) for _ in range(2)]
        self.rows_acc = [jnp.zeros((16, width), jnp.float32) for _ in range(3)]

    def add(self, l, east, west, north, south, fold):
        for i, col in enumerate((east, west)):
            wide = jnp.broadcast_to(col, (self.rows, TLON))
            self.cols[i] = jnp.where(self.lane == l, wide, self.cols[i])
        for i, line in enumerate((north, south, fold)):
            tall = jnp.broadcast_to(line, (16, self.width))
            self.rows_acc[i] = jnp.where(self.row == l, tall, self.rows_acc[i])

    def finish(self, pe_ref, pw_ref, pn_ref, ps_ref, pf_ref):
        levels = self.levels
        pe_ref[...] = self.cols[0][:, :levels]
        pw_ref[...] = self.cols[1][:, :levels]
        pn_ref[...] = self.rows_acc[0][:levels]
        ps_ref[...] = self.rows_acc[1][:levels]
        fold = self.rows_acc[2]
        if self.reverse_fold:
            fold = reverse_lanes(fold)
        pf_ref[...] = fold[:levels]

    def finish_pairs(self, n_lat, pe_ref, pw_ref, pa_ref, pb_ref):
        levels = self.levels
        pe_ref[...] = self.cols[0][:, :levels]
        pw_ref[...] = self.cols[1][:, :levels]
        north_going = self.rows_acc[0][:levels]
        south_going = self.rows_acc[1][:levels]
        fold = reverse_lanes(self.rows_acc[2])[:levels]
        even, top = lat_position(n_lat)
        pa_ref[...] = jnp.where(even, south_going, north_going)
        pb_ref[...] = jnp.where(top, fold, jnp.where(even, north_going, south_going))


def coefficients(l, d, u, v, rows, width):
    return (
        d[:, 0:1] + advect_scale * u[:, 0:1],
        d[:, width - 1:width] - advect_scale * u[:, width - 1:width],
        d[0:1, :] + advect_scale * v[0:1, :],
        d[rows - 1:rows, :] - advect_scale * v[rows - 1:rows, :],
        d[rows - 1:rows, :] + advect_scale * v[rows - 1:rows, :],
    )


def edge_values(ce, cw, cn, cs, cf, a, rows, width):
    return (
        ce * a[:, 0:1],
        cw * a[:, width - 1:width],
        cn * a[0:1, :],
        cs * a[rows - 1:rows, :],
        cf * a[rows - 1:rows, :],
    )


def prologue_kernel(n_lat, si_ref, wt_ref, af_ref, d_ref, u_ref, vlo_ref, vhi_ref, pe_ref, pw_ref, pa_ref, pb_ref):
    del si_ref
    levels, rows, width = af_ref.shape
    wet = wet_field(wt_ref, rows, width)
    d = d_ref[...]
    tile = vhi_ref.shape[1]
    out = Collector(levels, rows, width, True)
    for l in range(levels):
        u = u_ref[l]
        v_first = vlo_ref[l, 0:1, :]
        v_last = vhi_ref[l, tile - 1:tile, :]
        coef = (
            d[:, 0:1] + advect_scale * u[:, 0:1],
            d[:, width - 1:width] - advect_scale * u[:, width - 1:width],
            d[0:1, :] + advect_scale * v_first,
            d[rows - 1:rows, :] - advect_scale * v_last,
            d[rows - 1:rows, :] + advect_scale * v_last,
        )
        out.add(l, *edge_values(*coef, af_ref[l] * wet, rows, width))
    out.finish_pairs(n_lat, pe_ref, pw_ref, pa_ref, pb_ref)


def core_kernel(first, emit, si_ref, wt_ref, lm_ref, adj_ref, d_ref, t_ref, u_ref, v_ref, *rest):
    del si_ref
    if emit:
        u2_ref, v2_ref, out_ref, ce_ref, cw_ref, cn_ref, cs_ref, cf_ref, a_ref = rest
    else:
        out_ref, a_ref = rest
    levels, rows, width = adj_ref.shape
    lane = lax.broadcasted_iota(jnp.int32, (rows, width), 1)
    row = lax.broadcasted_iota(jnp.int32, (rows, width), 0)
    wet = wet_field(wt_ref, rows, width)
    if first:
        for m in range(levels):
            a_ref[m] = adj_ref[m] * wet
        src = a_ref
    else:
        src = adj_ref
    d = d_ref[...]
    coef = Collector(levels, rows, width, False) if emit else None

    for l in range(levels):
        a = src[l]
        vertical = lm_ref[0, l] * src[0]
        for m in range(1, levels):
            vertical = vertical + lm_ref[m, l] * src[m]
        s = d * a
        zf = u_ref[l] * a
        mf = v_ref[l] * a
        east = jnp.where(lane == width - 1, 0.0, pltpu.roll(s + advect_scale * zf, width - 1, 1))
        west = jnp.where(lane == 0, 0.0, pltpu.roll(s - advect_scale * zf, 1, 1))
        north = jnp.where(row == rows - 1, 0.0, pltpu.roll(s + advect_scale * mf, rows - 1, 0))
        south = jnp.where(row == 0, 0.0, pltpu.roll(s - advect_scale * mf, 1, 0))
        t = t_ref[l]
        out_ref[l] = wet * (a - 4.0 * s + east + west + north + south + vertical - damping * t * t * a)
        if emit:
            coef.add(l, *coefficients(l, d, u2_ref[l], v2_ref[l], rows, width))
    if emit:
        coef.finish(ce_ref, cw_ref, cn_ref, cs_ref, cf_ref)


def fix_kernel(emit, n_lat, wt_ref, part_ref, he_ref, hw_ref, ha_ref, hb_ref, *rest):
    if emit:
        ce_ref, cw_ref, cn_ref, cs_ref, cf_ref, out_ref, pe_ref, pw_ref, pa_ref, pb_ref = rest
    else:
        (out_ref,) = rest
    levels, rows, width = part_ref.shape
    wet = wet_field(wt_ref, rows, width)
    wet_left, wet_right = wet[:, :TLON], wet[:, width - TLON:]
    wet_bottom, wet_top = wet[0:1, :], wet[rows - 1:rows, :]
    lane = lax.broadcasted_iota(jnp.int32, (rows, TLON), 1)
    he = he_ref[...]
    hw = hw_ref[...]
    even, _ = lat_position(n_lat)
    if emit:
        ce = ce_ref[...]
        cw = cw_ref[...]
        out = Collector(levels, rows, width, True)
    for l in range(levels):
        x = part_ref[l]
        east = jnp.where(lane == TLON - 1, jnp.broadcast_to(he[:, l:l + 1], (rows, TLON)), 0.0)
        west = jnp.where(lane == 0, jnp.broadcast_to(hw[:, l:l + 1], (rows, TLON)), 0.0)
        out_ref[l] = x
        out_ref[l, :, width - TLON:] = x[:, width - TLON:] + wet_right * east
        out_ref[l, :, :TLON] = out_ref[l, :, :TLON] + wet_left * west
        a_row = ha_ref[l:l + 1, :]
        b_row = hb_ref[l:l + 1, :]
        north_row = jnp.where(even, a_row, b_row)
        south_row = jnp.where(even, b_row, a_row)
        out_ref[l, rows - 1:rows, :] = out_ref[l, rows - 1:rows, :] + wet_top * north_row
        out_ref[l, 0:1, :] = out_ref[l, 0:1, :] + wet_bottom * south_row
        if emit:
            new = out_ref[l]
            coef = (ce[:, l:l + 1], cw[:, l:l + 1], cn_ref[l:l + 1, :], cs_ref[l:l + 1, :], cf_ref[l:l + 1, :])
            out.add(l, *edge_values(*coef, new, rows, width))
    if emit:
        out.finish_pairs(n_lat, pe_ref, pw_ref, pa_ref, pb_ref)


def payload_shapes(levels, rows, width):
    lon = jax.ShapeDtypeStruct((rows, levels), jnp.float32)
    lat = jax.ShapeDtypeStruct((levels, width), jnp.float32)
    return [lon, lon, lat, lat, lat]


def pair_shapes(levels, rows, width):
    return payload_shapes(levels, rows, width)[:4]


def whole(shape):
    return pl.BlockSpec(shape, lambda i, *_: (0,) * len(shape))


def state_spec(k, levels, rows, width):
    return pl.BlockSpec((None, levels, rows, width), lambda i, si, *_: (si[k], 0, 0, 0))


def run_prologue(k, n_lat, si, wt, af, d, zonal, merid):
    levels, rows, width = af.shape
    shapes = pair_shapes(levels, rows, width)
    tile = 8
    last = rows // tile - 1
    v_lo = pl.BlockSpec((None, levels, tile, width), lambda i, si, *_: (si[k], 0, 0, 0))
    v_hi = pl.BlockSpec((None, levels, tile, width), lambda i, si, *_: (si[k], 0, last, 0))
    n = levels * rows * width
    return pl.pallas_call(
        functools.partial(prologue_kernel, n_lat),
        out_shape=shapes,
        grid_spec=pltpu.PrefetchScalarGridSpec(
            num_scalar_prefetch=2,
            grid=(1,),
            in_specs=[whole(af.shape), whole(d.shape), state_spec(k, levels, rows, width), v_lo, v_hi],
            out_specs=[whole(s.shape) for s in shapes],
        ),
        cost_estimate=pl.CostEstimate(flops=2 * n, bytes_accessed=10 * n, transcendentals=0),
    )(si, wt, af, d, zonal, merid, merid)


def run_core(k, k_next, si, wt, lm, adj, d, tracer, zonal, merid):
    levels, rows, width = adj.shape
    first = k_next is not None
    emit = k_next is not None
    state = state_spec(k, levels, rows, width)
    in_specs = [pl.BlockSpec(memory_space=pltpu.SMEM), whole(adj.shape), whole(d.shape), state, state, state]
    args = [si, wt, lm, adj, d, tracer, zonal, merid]
    out_shape = [jax.ShapeDtypeStruct(adj.shape, jnp.float32)]
    if emit:
        nxt = state_spec(k_next, levels, rows, width)
        in_specs += [nxt, nxt]
        args += [zonal, merid]
        out_shape += payload_shapes(levels, rows, width)
    n = levels * rows * width
    outs = pl.pallas_call(
        functools.partial(core_kernel, first, emit),
        out_shape=out_shape,
        grid_spec=pltpu.PrefetchScalarGridSpec(
            num_scalar_prefetch=2,
            grid=(1,),
            in_specs=in_specs,
            out_specs=[whole(s.shape) for s in out_shape],
            scratch_shapes=[pltpu.VMEM((levels, rows, width), jnp.float32)],
        ),
        cost_estimate=pl.CostEstimate(flops=60 * n, bytes_accessed=32 * n, transcendentals=0),
    )(*args)
    return outs[0], outs[1:]


def run_fix(n_lat, wt, part, halos, coefs):
    levels, rows, width = part.shape
    emit = bool(coefs)
    args = [wt, part, *halos, *coefs]
    in_specs = [whole(x.shape) for x in args[1:]]
    out_shape = [jax.ShapeDtypeStruct(part.shape, jnp.float32)]
    if emit:
        out_shape += pair_shapes(levels, rows, width)
    n = levels * rows * width
    outs = pl.pallas_call(
        functools.partial(fix_kernel, emit, n_lat),
        out_shape=out_shape,
        grid_spec=pltpu.PrefetchScalarGridSpec(
            num_scalar_prefetch=1,
            grid=(1,),
            in_specs=in_specs,
            out_specs=[whole(s.shape) for s in out_shape],
        ),
        cost_estimate=pl.CostEstimate(flops=10 * n, bytes_accessed=8 * n, transcendentals=0),
    )(*args)
    return outs[0], outs[1:]


def fix_in_xla(wet_tiles, lat_index, part, halos):
    levels, rows, width = part.shape
    he, hw, ha, hb = halos
    even = lat_index % 2 == 0
    north = jnp.where(even, ha, hb)
    south = jnp.where(even, hb, ha)
    wet = jnp.repeat(wet_tiles.reshape(-1), TLON).astype(jnp.float32)
    g = lax.broadcasted_iota(jnp.int32, part.shape, 2)
    r = lax.broadcasted_iota(jnp.int32, part.shape, 1)
    corr = (
        jnp.where(g == width - 1, he.T[:, :, None], 0.0)
        + jnp.where(g == 0, hw.T[:, :, None], 0.0)
        + jnp.where(r == rows - 1, north[:, None, :], 0.0)
        + jnp.where(r == 0, south[:, None, :], 0.0)
    )
    return part + wet * corr


def shards(
    adjoint_final,
    stored_tracer,
    stored_zonal,
    stored_meridional,
    diffusivity,
    level_mixing,
    wet_tiles,
    state_index,
):
    n_lat = lax.axis_size("lat")
    n_lon = lax.axis_size("lon")
    wt = wet_tiles.reshape(-1)
    lat_index = lax.axis_index("lat")

    to_west = shift_pairs(n_lon, -1, True)
    to_east = shift_pairs(n_lon, 1, True)
    pairs_a = [(i, i ^ 1) for i in range(n_lat)]
    top = n_lat - 1
    pairs_b = []
    for j in range(n_lon):
        for i in range(1, n_lat - 1, 2):
            pairs_b += [(j * n_lat + i, j * n_lat + i + 1), (j * n_lat + i + 1, j * n_lat + i)]
        pairs_b.append((j * n_lat + top, (n_lon - 1 - j) * n_lat + top))

    def exchange(payloads):
        pe, pw, pa, pb = payloads
        he = lax.ppermute(pe, "lon", to_west)
        hw = lax.ppermute(pw, "lon", to_east)
        ha = lax.ppermute(pa, "lat", pairs_a)
        hb = lax.ppermute(pb, ("lon", "lat"), pairs_b)
        return he, hw, ha, hb

    payloads = run_prologue(STEPS - 1, n_lat, state_index, wt, adjoint_final, diffusivity,
                            stored_zonal, stored_meridional)
    adj = adjoint_final
    for back in range(STEPS):
        k = STEPS - 1 - back
        k_next = k - 1 if k > 0 else None
        halos = exchange(payloads)
        part, coefs = run_core(k, k_next, state_index, wt, level_mixing, adj, diffusivity,
                               stored_tracer, stored_zonal, stored_meridional)
        if coefs:
            adj, payloads = run_fix(n_lat, wt, part, halos, coefs)
        else:
            adj = fix_in_xla(wet_tiles, lat_index, part, halos)
    return adj


def solution(mesh):
    return jax.shard_map(
        shards,
        mesh=mesh,
        in_specs=(
            P(None, "lat", "lon"),
            P(None, None, "lat", "lon"),
            P(None, None, "lat", "lon"),
            P(None, None, "lat", "lon"),
            P("lat", "lon"),
            P(),
            P("lat", "lon"),
            P(),
        ),
        out_specs=P(None, "lat", "lon"),
        check_vma=False,
    )
```

```python
import functools

import jax
import jax.numpy as jnp
from jax import lax
from jax.experimental import pallas as pl
from jax.experimental.pallas import tpu as pltpu
from jax.sharding import PartitionSpec as P


TLON = 128
STEPS = 2


advect_scale = 0.25
damping = 0.3


def shift_pairs(count, delta, periodic):
    pairs = []
    for i in range(count):
        j = i + delta
        if periodic:
            pairs.append((i, j % count))
        elif 0 <= j < count:
            pairs.append((i, j))
    return pairs


def wet_field(wt_ref, rows, width):
    lane = lax.broadcasted_iota(jnp.int32, (rows, width), 1)
    wet_i = jnp.zeros((rows, width), jnp.int32)
    for t in range(width // TLON):
        inside = (lane >= t * TLON) & (lane < (t + 1) * TLON)
        wet_i = jnp.where(inside, wt_ref[t], wet_i)
    return wet_i.astype(jnp.float32)


def reverse_lanes(x):
    width = x.shape[-1]
    i = lax.broadcasted_iota(jnp.int32, (width, width), 0)
    j = lax.broadcasted_iota(jnp.int32, (width, width), 1)
    flip = jnp.where(i + j == width - 1, 1.0, 0.0).astype(jnp.bfloat16)
    x1 = x.astype(jnp.bfloat16)
    r1 = x - x1.astype(jnp.float32)
    x2 = r1.astype(jnp.bfloat16)
    x3 = (r1 - x2.astype(jnp.float32)).astype(jnp.bfloat16)

    def perm(part):
        return jnp.dot(part, flip, preferred_element_type=jnp.float32)

    return (perm(x1) + perm(x2)) + perm(x3)


def lat_position(n_lat):
    lat = lax.axis_index("lat")
    return lat % 2 == 0, lat == n_lat - 1


class Collector:
    def __init__(self, levels, rows, width, reverse_fold):
        self.levels = levels
        self.rows = rows
        self.width = width
        self.reverse_fold = reverse_fold
        self.lane = lax.broadcasted_iota(jnp.int32, (rows, TLON), 1)
        self.row = lax.broadcasted_iota(jnp.int32, (16, width), 0)
        self.cols = [jnp.zeros((rows, TLON), jnp.float32) for _ in range(2)]
        self.rows_acc = [jnp.zeros((16, width), jnp.float32) for _ in range(3)]

    def add(self, l, east, west, north, south, fold):
        for i, col in enumerate((east, west)):
            wide = jnp.broadcast_to(col, (self.rows, TLON))
            self.cols[i] = jnp.where(self.lane == l, wide, self.cols[i])
        for i, line in enumerate((north, south, fold)):
            tall = jnp.broadcast_to(line, (16, self.width))
            self.rows_acc[i] = jnp.where(self.row == l, tall, self.rows_acc[i])

    def finish(self, pe_ref, pw_ref, pn_ref, ps_ref, pf_ref):
        levels = self.levels
        pe_ref[...] = self.cols[0][:, :levels]
        pw_ref[...] = self.cols[1][:, :levels]
        pn_ref[...] = self.rows_acc[0][:levels]
        ps_ref[...] = self.rows_acc[1][:levels]
        fold = self.rows_acc[2]
        if self.reverse_fold:
            fold = reverse_lanes(fold)
        pf_ref[...] = fold[:levels]

    def finish_pairs(self, n_lat, pe_ref, pw_ref, pa_ref, pb_ref):
        levels = self.levels
        pe_ref[...] = self.cols[0][:, :levels]
        pw_ref[...] = self.cols[1][:, :levels]
        north_going = self.rows_acc[0][:levels]
        south_going = self.rows_acc[1][:levels]
        fold = reverse_lanes(self.rows_acc[2])[:levels]
        even, top = lat_position(n_lat)
        pa_ref[...] = jnp.where(even, south_going, north_going)
        pb_ref[...] = jnp.where(top, fold, jnp.where(even, north_going, south_going))


def coefficients(d, u, v, rows, width):
    return (
        d[:, 0:1] + advect_scale * u[:, 0:1],
        d[:, width - 1:width] - advect_scale * u[:, width - 1:width],
        d[0:1, :] + advect_scale * v[0:1, :],
        d[rows - 1:rows, :] - advect_scale * v[rows - 1:rows, :],
        d[rows - 1:rows, :] + advect_scale * v[rows - 1:rows, :],
    )


def edge_values(ce, cw, cn, cs, cf, a, rows, width):
    return (
        ce * a[:, 0:1],
        cw * a[:, width - 1:width],
        cn * a[0:1, :],
        cs * a[rows - 1:rows, :],
        cf * a[rows - 1:rows, :],
    )


def prologue_kernel(n_lat, si_ref, wt_ref, af_ref, d_ref, u_ref, vlo_ref, vhi_ref, pe_ref, pw_ref, pa_ref, pb_ref):
    del si_ref
    levels, rows, width = af_ref.shape
    wet = wet_field(wt_ref, rows, width)
    d = d_ref[...]
    tile = vhi_ref.shape[1]
    out = Collector(levels, rows, width, True)
    for l in range(levels):
        u = u_ref[l]
        v_first = vlo_ref[l, 0:1, :]
        v_last = vhi_ref[l, tile - 1:tile, :]
        coef = (
            d[:, 0:1] + advect_scale * u[:, 0:1],
            d[:, width - 1:width] - advect_scale * u[:, width - 1:width],
            d[0:1, :] + advect_scale * v_first,
            d[rows - 1:rows, :] - advect_scale * v_last,
            d[rows - 1:rows, :] + advect_scale * v_last,
        )
        out.add(l, *edge_values(*coef, af_ref[l] * wet, rows, width))
    out.finish_pairs(n_lat, pe_ref, pw_ref, pa_ref, pb_ref)


def core_kernel(first, emit, si_ref, wt_ref, lm_ref, adj_ref, d_ref, t_ref, u_ref, v_ref, *rest):
    del si_ref
    if emit:
        u2_ref, v2_ref, out_ref, ce_ref, cw_ref, cn_ref, cs_ref, cf_ref, a_ref = rest
    else:
        out_ref, a_ref = rest
    levels, rows, width = adj_ref.shape
    lane = lax.broadcasted_iota(jnp.int32, (rows, width), 1)
    row = lax.broadcasted_iota(jnp.int32, (rows, width), 0)
    wet = wet_field(wt_ref, rows, width)
    if first:
        for m in range(levels):
            a_ref[m] = adj_ref[m] * wet
        src = a_ref
    else:
        src = adj_ref
    d = d_ref[...]
    coef = Collector(levels, rows, width, False) if emit else None

    for l in range(levels):
        a = src[l]
        vertical = lm_ref[0, l] * src[0]
        for m in range(1, levels):
            vertical = vertical + lm_ref[m, l] * src[m]
        s = d * a
        zf = u_ref[l] * a
        mf = v_ref[l] * a
        east = jnp.where(lane == width - 1, 0.0, pltpu.roll(s + advect_scale * zf, width - 1, 1))
        west = jnp.where(lane == 0, 0.0, pltpu.roll(s - advect_scale * zf, 1, 1))
        north = jnp.where(row == rows - 1, 0.0, pltpu.roll(s + advect_scale * mf, rows - 1, 0))
        south = jnp.where(row == 0, 0.0, pltpu.roll(s - advect_scale * mf, 1, 0))
        t = t_ref[l]
        out_ref[l] = wet * (a - 4.0 * s + east + west + north + south + vertical - damping * t * t * a)
        if emit:
            coef.add(l, *coefficients(d, u2_ref[l], v2_ref[l], rows, width))
    if emit:
        coef.finish(ce_ref, cw_ref, cn_ref, cs_ref, cf_ref)


def fix_kernel(emit, n_lat, wt_ref, part_ref, he_ref, hw_ref, ha_ref, hb_ref, *rest):
    if emit:
        ce_ref, cw_ref, cn_ref, cs_ref, cf_ref, out_ref, pe_ref, pw_ref, pa_ref, pb_ref = rest
    else:
        (out_ref,) = rest
    levels, rows, width = part_ref.shape
    wet = wet_field(wt_ref, rows, width)
    wet_left, wet_right = wet[:, :TLON], wet[:, width - TLON:]
    wet_bottom, wet_top = wet[0:1, :], wet[rows - 1:rows, :]
    lane = lax.broadcasted_iota(jnp.int32, (rows, TLON), 1)
    he = he_ref[...]
    hw = hw_ref[...]
    even, _ = lat_position(n_lat)
    if emit:
        ce = ce_ref[...]
        cw = cw_ref[...]
        out = Collector(levels, rows, width, True)
    for l in range(levels):
        x = part_ref[l]
        east = jnp.where(lane == TLON - 1, jnp.broadcast_to(he[:, l:l + 1], (rows, TLON)), 0.0)
        west = jnp.where(lane == 0, jnp.broadcast_to(hw[:, l:l + 1], (rows, TLON)), 0.0)
        out_ref[l] = x
        out_ref[l, :, width - TLON:] = x[:, width - TLON:] + wet_right * east
        out_ref[l, :, :TLON] = out_ref[l, :, :TLON] + wet_left * west
        a_row = ha_ref[l:l + 1, :]
        b_row = hb_ref[l:l + 1, :]
        north_row = jnp.where(even, a_row, b_row)
        south_row = jnp.where(even, b_row, a_row)
        out_ref[l, rows - 1:rows, :] = out_ref[l, rows - 1:rows, :] + wet_top * north_row
        out_ref[l, 0:1, :] = out_ref[l, 0:1, :] + wet_bottom * south_row
        if emit:
            new = out_ref[l]
            coef = (ce[:, l:l + 1], cw[:, l:l + 1], cn_ref[l:l + 1, :], cs_ref[l:l + 1, :], cf_ref[l:l + 1, :])
            out.add(l, *edge_values(*coef, new, rows, width))
    if emit:
        out.finish_pairs(n_lat, pe_ref, pw_ref, pa_ref, pb_ref)


def payload_shapes(levels, rows, width):
    lon = jax.ShapeDtypeStruct((rows, levels), jnp.float32)
    lat = jax.ShapeDtypeStruct((levels, width), jnp.float32)
    return [lon, lon, lat, lat, lat]


def pair_shapes(levels, rows, width):
    return payload_shapes(levels, rows, width)[:4]


def whole(shape):
    return pl.BlockSpec(shape, lambda i, *_: (0,) * len(shape))


def state_spec(k, levels, rows, width):
    return pl.BlockSpec((None, levels, rows, width), lambda i, si, *_: (si[k], 0, 0, 0))


def run_prologue(k, n_lat, si, wt, af, d, zonal, merid):
    levels, rows, width = af.shape
    shapes = pair_shapes(levels, rows, width)
    tile = 8
    last = rows // tile - 1
    v_lo = pl.BlockSpec((None, levels, tile, width), lambda i, si, *_: (si[k], 0, 0, 0))
    v_hi = pl.BlockSpec((None, levels, tile, width), lambda i, si, *_: (si[k], 0, last, 0))
    n = levels * rows * width
    return pl.pallas_call(
        functools.partial(prologue_kernel, n_lat),
        out_shape=shapes,
        grid_spec=pltpu.PrefetchScalarGridSpec(
            num_scalar_prefetch=2,
            grid=(1,),
            in_specs=[whole(af.shape), whole(d.shape), state_spec(k, levels, rows, width), v_lo, v_hi],
            out_specs=[whole(s.shape) for s in shapes],
        ),
        cost_estimate=pl.CostEstimate(flops=2 * n, bytes_accessed=10 * n, transcendentals=0),
    )(si, wt, af, d, zonal, merid, merid)


def run_core(k, k_next, si, wt, lm, adj, d, tracer, zonal, merid):
    levels, rows, width = adj.shape
    first = k_next is not None
    emit = k_next is not None
    state = state_spec(k, levels, rows, width)
    in_specs = [pl.BlockSpec(memory_space=pltpu.SMEM), whole(adj.shape), whole(d.shape), state, state, state]
    args = [si, wt, lm, adj, d, tracer, zonal, merid]
    out_shape = [jax.ShapeDtypeStruct(adj.shape, jnp.float32)]
    if emit:
        nxt = state_spec(k_next, levels, rows, width)
        in_specs += [nxt, nxt]
        args += [zonal, merid]
        out_shape += payload_shapes(levels, rows, width)
    n = levels * rows * width
    outs = pl.pallas_call(
        functools.partial(core_kernel, first, emit),
        out_shape=out_shape,
        grid_spec=pltpu.PrefetchScalarGridSpec(
            num_scalar_prefetch=2,
            grid=(1,),
            in_specs=in_specs,
            out_specs=[whole(s.shape) for s in out_shape],
            scratch_shapes=[pltpu.VMEM((levels, rows, width), jnp.float32)],
        ),
        cost_estimate=pl.CostEstimate(flops=60 * n, bytes_accessed=32 * n, transcendentals=0),
    )(*args)
    return outs[0], outs[1:]


def run_fix(n_lat, wt, part, halos, coefs):
    levels, rows, width = part.shape
    emit = bool(coefs)
    args = [wt, part, *halos, *coefs]
    in_specs = [whole(x.shape) for x in args[1:]]
    out_shape = [jax.ShapeDtypeStruct(part.shape, jnp.float32)]
    if emit:
        out_shape += pair_shapes(levels, rows, width)
    n = levels * rows * width
    outs = pl.pallas_call(
        functools.partial(fix_kernel, emit, n_lat),
        out_shape=out_shape,
        grid_spec=pltpu.PrefetchScalarGridSpec(
            num_scalar_prefetch=1,
            grid=(1,),
            in_specs=in_specs,
            out_specs=[whole(s.shape) for s in out_shape],
        ),
        cost_estimate=pl.CostEstimate(flops=10 * n, bytes_accessed=8 * n, transcendentals=0),
    )(*args)
    return outs[0], outs[1:]


def fix_in_xla(wet_tiles, lat_index, part, halos):
    _, rows, width = part.shape
    he, hw, ha, hb = halos
    even = lat_index % 2 == 0
    north = jnp.where(even, ha, hb)
    south = jnp.where(even, hb, ha)
    wet = jnp.repeat(wet_tiles.reshape(-1), TLON).astype(jnp.float32)
    g = lax.broadcasted_iota(jnp.int32, part.shape, 2)
    r = lax.broadcasted_iota(jnp.int32, part.shape, 1)
    corr = (
        jnp.where(g == width - 1, he.T[:, :, None], 0.0)
        + jnp.where(g == 0, hw.T[:, :, None], 0.0)
        + jnp.where(r == rows - 1, north[:, None, :], 0.0)
        + jnp.where(r == 0, south[:, None, :], 0.0)
    )
    return part + wet * corr


def shards(
    adjoint_final,
    stored_tracer,
    stored_zonal,
    stored_meridional,
    diffusivity,
    level_mixing,
    wet_tiles,
    state_index,
):
    n_lat = lax.axis_size("lat")
    n_lon = lax.axis_size("lon")
    wt = wet_tiles.reshape(-1)
    lat_index = lax.axis_index("lat")

    to_west = shift_pairs(n_lon, -1, True)
    to_east = shift_pairs(n_lon, 1, True)
    pairs_a = [(i, i ^ 1) for i in range(n_lat)]
    top = n_lat - 1
    pairs_b = []
    for j in range(n_lon):
        for i in range(1, n_lat - 1, 2):
            pairs_b += [(j * n_lat + i, j * n_lat + i + 1), (j * n_lat + i + 1, j * n_lat + i)]
        pairs_b.append((j * n_lat + top, (n_lon - 1 - j) * n_lat + top))

    def exchange(payloads):
        pe, pw, pa, pb = payloads
        hb = lax.ppermute(pb, ("lon", "lat"), pairs_b)
        ha = lax.ppermute(pa, "lat", pairs_a)
        he = lax.ppermute(pe, "lon", to_west)
        hw = lax.ppermute(pw, "lon", to_east)
        return he, hw, ha, hb

    payloads = run_prologue(STEPS - 1, n_lat, state_index, wt, adjoint_final, diffusivity,
                            stored_zonal, stored_meridional)
    adj = adjoint_final
    for back in range(STEPS):
        k = STEPS - 1 - back
        k_next = k - 1 if k > 0 else None
        halos = exchange(payloads)
        part, coefs = run_core(k, k_next, state_index, wt, level_mixing, adj, diffusivity,
                               stored_tracer, stored_zonal, stored_meridional)
        if coefs:
            adj, payloads = run_fix(n_lat, wt, part, halos, coefs)
        else:
            adj = fix_in_xla(wet_tiles, lat_index, part, halos)
    return adj


def solution(mesh):
    return jax.shard_map(
        shards,
        mesh=mesh,
        in_specs=(
            P(None, "lat", "lon"),
            P(None, None, "lat", "lon"),
            P(None, None, "lat", "lon"),
            P(None, None, "lat", "lon"),
            P("lat", "lon"),
            P(),
            P("lat", "lon"),
            P(),
        ),
        out_specs=P(None, "lat", "lon"),
        check_vma=False,
    )
```
